128 devices in a mesh: dp: 8 (over x, core), seq: 16 (over z, y).
Axes of the slice: x: 4, y: 4, z: 4, core: 2. Of those that a mesh axis runs over, the one named last changes fastest.
Arguments:
- queries: bfloat16 [16384, 4096], P(('dp', 'seq')), may hold values from -5 to 5
- key_states: bfloat16 [16384, 512], P(('dp', 'seq')), may hold values from -5 to 5
- value_states: bfloat16 [16384, 512], P(('dp', 'seq')), may hold values from -6 to 6
- grad_out: bfloat16 [16384, 4096], P(('dp', 'seq')), may hold values from -6 to 6
- doc_lengths: int32 [32], replicated, may hold values from 1 to 2048, 16384 in all
Outputs:
- grad_queries: bfloat16 [16384, 4096], P(('dp', 'seq'))
- grad_keys: bfloat16 [16384, 512], P(('dp', 'seq'))
- grad_values: bfloat16 [16384, 512], P(('dp', 'seq'))
The draws below stay inside these ranges and needn't reach their ends.
Inputs may be any that keep to these rules, and one draw needn't show every extreme that they name: `doc_lengths`: 32 documents packed in order, lengths summing to 16384; one document has exactly 2048 tokens.
All inputs are finite; a program needn't handle non-finite values.
Results may differ from the reference program's by a relative error of at most 0.014.
Values may be sent and summed in bfloat16 or wider, within the bound.
No kernel may reach another device: no remote copies, remote signals or barrier semaphores. Data moves between devices by JAX's collectives and lax.ppermute only.
A program may use at most 256 MiB of HBM per device.

```python
import math
import jax
import jax.numpy as jnp
import numpy as np
from jax import lax

QH = 32
KVH = 4
HD = 128
TOKENS = 16384
MAX_DOC = 2048
QB = 512
DOCS = 32


def drawn_draw(key, columns):
    values = jnp.clip(jax.random.normal(key, (TOKENS, columns), jnp.float32), -4.5, 4.5)
    return values


def draw_key_states(key, part):
    values = drawn_draw(jax.random.fold_in(key, 1), KVH * HD)
    return values.astype(jnp.bfloat16)


def draw_queries(key, part):
    values = drawn_draw(jax.random.fold_in(key, 2), QH * HD)
    return values.astype(jnp.bfloat16)


def block_scale(rng, dims, shards, low, largest):
    factor_of, own = 1.0, jax.random.fold_in(rng, 6)
    for axis_at, shards_of in shards:
        steps = jnp.exp(jax.random.uniform(jax.random.fold_in(own, axis_at), (shards_of,), jnp.float32, low / len(shards), largest / len(shards)))
        factor_of = factor_of * jnp.repeat(steps, dims[axis_at] // shards_of).reshape([-1 if axis == axis_at else 1 for axis in range(len(dims))])
    return factor_of


def length_profile(amount, total, limit, lean):
    weights = [(1 << 20) // math.isqrt(rank ** lean) + 1 for rank in range(2, amount + 1)]
    surplus, given = total - limit - (amount - 1), [1] * (amount - 1)
    while surplus > 0:
        movable = [i for i in range(amount - 1) if given[i] < limit]
        whole, budget = sum([weights[i] for i in movable]), surplus
        for i in movable:
            addition = min(limit - given[i], max(1, budget * weights[i] // whole), surplus)
            given[i] = given[i] + addition
            surplus = surplus - addition
    return np.array([limit] + given)


def uneven_parts(rng, count, total, limit, slope):
    if count == 2:
        one = jax.random.randint(rng, (), max(1, total - limit), min(limit, total - 1) + 1)
        return jnp.stack([one, total - one])
    sizes = jnp.asarray(length_profile(count, total, limit, slope), jnp.int32)
    twos = (count - 1) // 2
    donor, receiver = sizes[1:1 + 2 * twos:2], sizes[2:2 + 2 * twos:2]
    room = jnp.minimum(donor - 1, limit - receiver)
    shifted = jax.random.randint(jax.random.fold_in(rng, 1), (twos,), 0, 1 << 20) % (room + 1)
    sizes = sizes.at[1:1 + 2 * twos:2].set(donor - shifted).at[2:2 + 2 * twos:2].set(receiver + shifted)
    return sizes[jax.random.permutation(jax.random.fold_in(rng, 2), count)]


def bell_draw(key, dims, scale, most, shards=(), kind=jnp.bfloat16):
    drawn = scale * jax.random.normal(key, dims, jnp.float32)
    if shards:
        drawn = drawn * block_scale(key, dims, shards, -0.22, 0.18)
    return jnp.clip(drawn, -most, most).astype(kind)


def setup_inputs(seed: int = 0) -> dict:
    arg_keys = jax.random.split(jax.random.key(seed), 6)
    queries = draw_queries(jax.random.fold_in(arg_keys[5], 71), 0)
    key_states = draw_key_states(jax.random.fold_in(arg_keys[5], 71), 0)
    value_states = bell_draw(arg_keys[2], (TOKENS, KVH * HD), 1.0, 6.0, ((0, 128),))
    grad_out = bell_draw(arg_keys[3], (TOKENS, QH * HD), 1.0, 6.0, ((0, 128),))
    doc_lengths = uneven_parts(arg_keys[4], DOCS, TOKENS, MAX_DOC, 2).astype(jnp.int32)
    return dict(queries=queries, key_states=key_states, value_states=value_states, grad_out=grad_out, doc_lengths=doc_lengths)


def doc_index(doc_lengths, positions):
    ends = jnp.cumsum(doc_lengths).astype(jnp.int32)
    counted = jnp.sum((ends[None, :] <= positions[:, None]).astype(jnp.int32), axis=1)
    return jnp.where(positions < 0, -1, counted).astype(jnp.int32)


def block_grads(query_blk, grad_blk, key_win, value_win, doc_query, pos_query, doc_key, pos_key):
    scaling = HD ** -0.5
    scores = jnp.einsum("qkgd,wkd->kgqw", query_blk, key_win) * scaling
    allowed = (doc_query[:, None] == doc_key[None, :]) & (pos_key[None, :] <= pos_query[:, None])
    row_max = jnp.max(jnp.where(allowed, scores, -jnp.inf), axis=-1, keepdims=True)
    numerator = jnp.where(allowed, jnp.exp(scores - row_max), 0.0)
    attn_prob = numerator / jnp.sum(numerator, axis=-1, keepdims=True)
    grad_prob = jnp.einsum("qkgd,wkd->kgqw", grad_blk, value_win)
    row_term = jnp.sum(attn_prob * grad_prob, axis=-1, keepdims=True)
    grad_score = (attn_prob * (grad_prob - row_term) * scaling).astype(jnp.bfloat16).astype(jnp.float32)
    prob_round = attn_prob.astype(jnp.bfloat16).astype(jnp.float32)
    grad_query = jnp.einsum("kgqw,wkd->qkgd", grad_score, key_win)
    grad_key = jnp.einsum("kgqw,qkgd->wkd", grad_score, query_blk)
    grad_value = jnp.einsum("kgqw,qkgd->wkd", prob_round, grad_blk)
    return grad_query, grad_key, grad_value


def reference(queries, key_states, value_states, grad_out, doc_lengths):
    per_group = QH // KVH
    width = MAX_DOC + QB
    query_four = queries.astype(jnp.float32).reshape(TOKENS, KVH, per_group, HD)
    grad_four = grad_out.astype(jnp.float32).reshape(TOKENS, KVH, per_group, HD)
    padding = ((MAX_DOC, 0), (0, 0), (0, 0))
    key_pad = jnp.pad(key_states.astype(jnp.float32).reshape(TOKENS, KVH, HD), padding)
    value_pad = jnp.pad(value_states.astype(jnp.float32).reshape(TOKENS, KVH, HD), padding)
    positions = jnp.arange(TOKENS, dtype=jnp.int32)
    doc_tokens = doc_index(doc_lengths, positions)
    pos_padded = jnp.arange(TOKENS + MAX_DOC, dtype=jnp.int32) - MAX_DOC
    doc_padded = doc_index(doc_lengths, pos_padded)

    def step(carry, block):
        key_acc, value_acc = carry
        first = (block * QB).astype(jnp.int32)
        query_blk = lax.dynamic_slice_in_dim(query_four, first, QB, 0)
        grad_blk = lax.dynamic_slice_in_dim(grad_four, first, QB, 0)
        key_win = lax.dynamic_slice_in_dim(key_pad, first, width, 0)
        value_win = lax.dynamic_slice_in_dim(value_pad, first, width, 0)
        doc_query = lax.dynamic_slice_in_dim(doc_tokens, first, QB, 0)
        pos_query = lax.dynamic_slice_in_dim(positions, first, QB, 0)
        doc_key = lax.dynamic_slice_in_dim(doc_padded, first, width, 0)
        pos_key = lax.dynamic_slice_in_dim(pos_padded, first, width, 0)
        grad_query, grad_key, grad_value = block_grads(query_blk, grad_blk, key_win, value_win, doc_query, pos_query, doc_key, pos_key)
        start = (first, jnp.int32(0), jnp.int32(0))
        key_acc = lax.dynamic_update_slice(key_acc, lax.dynamic_slice_in_dim(key_acc, first, width, 0) + grad_key, start)
        value_acc = lax.dynamic_update_slice(value_acc, lax.dynamic_slice_in_dim(value_acc, first, width, 0) + grad_value, start)
        return (key_acc, value_acc), grad_query.astype(jnp.bfloat16)

    zeros_acc = jnp.zeros((TOKENS + MAX_DOC, KVH, HD), jnp.float32)
    (key_acc, value_acc), query_blocks = lax.scan(step, (zeros_acc, zeros_acc), jnp.arange(TOKENS // QB, dtype=jnp.int32))
    grad_queries = query_blocks.reshape(TOKENS, QH * HD)
    grad_keys = key_acc[MAX_DOC:].reshape(TOKENS, KVH * HD).astype(jnp.bfloat16)
    grad_values = value_acc[MAX_DOC:].reshape(TOKENS, KVH * HD).astype(jnp.bfloat16)
    return (grad_queries, grad_keys, grad_values)
```

```python
import functools

import jax
import jax.numpy as jnp
from jax import lax
from jax.experimental import pallas as pl
from jax.experimental.pallas import tpu as pltpu
from jax.sharding import PartitionSpec as P

KVH = 4
HD = 128
BQ = 512
BK = 512
NEG = -1e30


def from_behind(value, axis, steps):
    count = lax.axis_size(axis)
    initial, last = (max(0, -steps), min(count, count - steps))
    return lax.ppermute(value, axis, [(source, source + steps) for source in range(initial, last)])


def expand_heads(states, repeat):
    rows = states.shape[0]
    grouped = states.reshape(rows, KVH, HD)
    return jnp.repeat(grouped, repeat, axis=1).reshape(rows, KVH * repeat * HD)


def dot_t(a, b):
    return lax.dot_general(a, b, (((1,), (1,)), ((), ())), preferred_element_type=jnp.float32)


def attend_kernel(
    tile_lo_ref, mixed_ref, rim_ref, lo_ref, dq_ref, dk_ref, dv_ref, dq_acc, m_scr, l_scr, dl_scr
):
    group = mixed_ref.shape[0]
    heads = dq_ref.shape[1] // HD
    rim_tiles = group // BK
    scale = HD ** (-0.5)
    kcol = 2 * heads * HD
    vcol = kcol + HD
    dk_ref[...] = jnp.zeros(dk_ref.shape, jnp.float32)
    dv_ref[...] = jnp.zeros(dv_ref.shape, jnp.float32)

    for h in range(heads):
        qcol = h * HD
        gcol = heads * HD + h * HD

        def query_tile(t, carry, qcol=qcol, gcol=gcol):
            qs = pl.multiple_of(t * BQ, BQ)
            q_blk = mixed_ref[pl.ds(qs, BQ), qcol : qcol + HD]
            g_blk = mixed_ref[pl.ds(qs, BQ), gcol : gcol + HD]
            lo = lo_ref[pl.ds(qs, BQ), :]
            q_pos = group + qs + lax.broadcasted_iota(jnp.int32, (BQ, BK), 0)
            kt_lo = tile_lo_ref[t]
            kt_hi = rim_tiles + (qs + BQ - 1) // BK

            def allowed_at(kt):
                k_pos = kt * BK + lax.broadcasted_iota(jnp.int32, (BQ, BK), 1)
                return (k_pos >= lo) & (k_pos <= q_pos)

            def sweep(step):
                def rim_step(kt, c):
                    row = pl.multiple_of(kt * BK, BK)
                    step(kt, rim_ref[pl.ds(row, BK), 0:HD], rim_ref[pl.ds(row, BK), HD : 2 * HD])
                    return c

                def own_step(kt, c):
                    row = pl.multiple_of((kt - rim_tiles) * BK, BK)
                    step(
                        kt,
                        mixed_ref[pl.ds(row, BK), kcol : kcol + HD],
                        mixed_ref[pl.ds(row, BK), vcol : vcol + HD],
                    )
                    return c

                lax.fori_loop(kt_lo, rim_tiles, rim_step, 0)
                lax.fori_loop(jnp.maximum(kt_lo, rim_tiles), kt_hi + 1, own_step, 0)

            def forward_step(kt, k_blk, v_blk):
                s = dot_t(q_blk, k_blk) * scale
                s = jnp.where(allowed_at(kt), s, NEG)
                dp = dot_t(g_blk, v_blk)
                m_old = m_scr[...]
                m_new = jnp.maximum(m_old, jnp.max(s, axis=1, keepdims=True))
                alpha = jnp.exp(m_old - m_new)
                p = jnp.exp(s - m_new)
                l_scr[...] = alpha * l_scr[...] + jnp.sum(p, axis=1, keepdims=True)
                dl_scr[...] = alpha * dl_scr[...] + jnp.sum(p * dp, axis=1, keepdims=True)
                m_scr[...] = m_new

            m_scr[...] = jnp.full(m_scr.shape, NEG, jnp.float32)
            l_scr[...] = jnp.zeros(l_scr.shape, jnp.float32)
            dl_scr[...] = jnp.zeros(dl_scr.shape, jnp.float32)
            sweep(forward_step)
            inv_l = 1.0 / l_scr[...]
            l_scr[...] = inv_l
            dl_scr[...] = dl_scr[...] * inv_l
            dq_acc[...] = jnp.zeros(dq_acc.shape, jnp.float32)

            def backward_step(kt, k_blk, v_blk):
                s = dot_t(q_blk, k_blk) * scale
                prob = jnp.where(allowed_at(kt), jnp.exp(s - m_scr[...]) * l_scr[...], 0.0)
                dp = dot_t(g_blk, v_blk)
                ds = (prob * (dp - dl_scr[...]) * scale).astype(jnp.bfloat16)
                dq_acc[...] += jnp.dot(ds, k_blk, preferred_element_type=jnp.float32)
                row = pl.multiple_of(kt * BK, BK)
                dk_ref[pl.ds(row, BK), :] += jnp.dot(
                    ds.T, q_blk, preferred_element_type=jnp.float32
                )
                dv_ref[pl.ds(row, BK), :] += jnp.dot(
                    prob.astype(jnp.bfloat16).T, g_blk, preferred_element_type=jnp.float32
                )

            sweep(backward_step)
            dq_ref[pl.ds(qs, BQ), qcol : qcol + HD] = dq_acc[...].astype(dq_ref.dtype)
            return carry

        lax.fori_loop(0, group // BQ, query_tile, 0)


def attend(tile_lo, mixed, rim, lo, heads, interpret=False):
    group = mixed.shape[0]
    vmem = pltpu.MemorySpace.VMEM if hasattr(pltpu, "MemorySpace") else pltpu.VMEM
    return pl.pallas_call(
        attend_kernel,
        out_shape=(
            jax.ShapeDtypeStruct((group, heads * HD), jnp.bfloat16),
            jax.ShapeDtypeStruct((2 * group, HD), jnp.float32),
            jax.ShapeDtypeStruct((2 * group, HD), jnp.float32),
        ),
        in_specs=[
            pl.BlockSpec(memory_space=pltpu.SMEM),
            pl.BlockSpec(memory_space=vmem),
            pl.BlockSpec(memory_space=vmem),
            pl.BlockSpec(memory_space=vmem),
        ],
        out_specs=(
            pl.BlockSpec(memory_space=vmem),
            pl.BlockSpec(memory_space=vmem),
            pl.BlockSpec(memory_space=vmem),
        ),
        scratch_shapes=[
            pltpu.VMEM((BQ, HD), jnp.float32),
            pltpu.VMEM((BQ, 1), jnp.float32),
            pltpu.VMEM((BQ, 1), jnp.float32),
            pltpu.VMEM((BQ, 1), jnp.float32),
        ],
        compiler_params=pltpu.CompilerParams(vmem_limit_bytes=48 * 1024 * 1024),
        interpret=interpret,
    )(tile_lo, mixed, rim, lo)


def doc_starts(doc_lengths, positions):
    ends = jnp.cumsum(doc_lengths)
    starts = ends - doc_lengths
    return jnp.max(jnp.where(starts[None, :] <= positions[:, None], starts[None, :], 0), axis=1)


def body(queries, key_states, value_states, grad_out, doc_lengths):
    seq_count = lax.axis_size("seq")
    repeat = max(1, seq_count // KVH)
    rows = queries.shape[0]
    packed = jnp.concatenate(
        [
            queries.reshape(rows, seq_count, -1),
            grad_out.reshape(rows, seq_count, -1),
            expand_heads(key_states, repeat).reshape(rows, seq_count, -1),
            expand_heads(value_states, repeat).reshape(rows, seq_count, -1),
        ],
        axis=2,
    ).reshape(rows, -1)
    mixed = lax.all_to_all(packed, "seq", split_axis=1, concat_axis=0, tiled=True)
    group = mixed.shape[0]
    heads = queries.shape[1] // (seq_count * HD)
    kcol = 2 * heads * HD
    rim = from_behind(mixed[:, kcol : kcol + 2 * HD], "dp", 1)
    root = lax.axis_index("dp") * group
    positions = root + jnp.arange(group, dtype=jnp.int32)
    lo = (doc_starts(doc_lengths, positions) - root + group).astype(jnp.int32)
    tile_lo = lo[::BQ] // BK
    dq, dk, dv = attend(tile_lo, mixed, rim, lo.reshape(group, 1), heads)
    rim_grad = jnp.concatenate([dk[:group], dv[:group]], axis=1).astype(jnp.bfloat16)
    back = from_behind(rim_grad, "dp", -1).astype(jnp.float32)
    own = (jnp.concatenate([dk[group:], dv[group:]], axis=1) + back).astype(jnp.bfloat16)
    out_packed = jnp.concatenate([dq, own], axis=1)
    returned = lax.all_to_all(out_packed, "seq", split_axis=0, concat_axis=1, tiled=True)
    returned = returned.reshape(rows, seq_count, -1)
    qw = heads * HD
    grad_queries = returned[:, :, :qw].reshape(rows, seq_count * qw)

    def fold(part):
        total = jnp.sum(part.astype(jnp.float32).reshape(rows, KVH, repeat, HD), axis=2)
        return total.reshape(rows, KVH * HD).astype(jnp.bfloat16)

    grad_keys = fold(returned[:, :, qw : qw + HD])
    grad_values = fold(returned[:, :, qw + HD : qw + 2 * HD])
    return (grad_queries, grad_keys, grad_values)


def solution(mesh):
    return jax.shard_map(
        body,
        mesh=mesh,
        in_specs=(
            P(("dp", "seq"), None),
            P(("dp", "seq"), None),
            P(("dp", "seq"), None),
            P(("dp", "seq"), None),
            P(),
        ),
        out_specs=(P(("dp", "seq"), None), P(("dp", "seq"), None), P(("dp", "seq"), None)),
        check_vma=False,
    )
```

```python
import functools

import jax
import jax.numpy as jnp
from jax import lax
from jax.experimental import pallas as pl
from jax.experimental.pallas import tpu as pltpu
from jax.sharding import PartitionSpec as P

KVH = 4
HD = 128
BQ = 512
BK = 512
NEG = -1e30


def from_behind(value, axis, steps):
    count = lax.axis_size(axis)
    initial, last = (max(0, -steps), min(count, count - steps))
    return lax.ppermute(value, axis, [(source, source + steps) for source in range(initial, last)])


def expand_heads(states, repeat):
    rows = states.shape[0]
    grouped = states.reshape(rows, KVH, HD)
    return jnp.repeat(grouped, repeat, axis=1).reshape(rows, KVH * repeat * HD)


def dot_t(a, b):
    return lax.dot_general(a, b, (((1,), (1,)), ((), ())), preferred_element_type=jnp.float32)


def attend_kernel(bounds_ref, mixed_ref, kv_ref, kt_ref, lo_ref, dq_ref, dk_ref, dv_ref, dq_acc, m_scr, l_scr, dl_scr):
    group = mixed_ref.shape[0]
    heads = dq_ref.shape[1] // HD
    tiles = group // BQ
    rim_tiles = group // BK
    scale = HD ** (-0.5)
    dk_ref[...] = jnp.zeros(dk_ref.shape, jnp.float32)
    dv_ref[...] = jnp.zeros(dv_ref.shape, jnp.float32)

    for h in range(heads):
        qcol = h * HD
        gcol = heads * HD + h * HD

        def query_tile(t, carry, qcol=qcol, gcol=gcol):
            qs = pl.multiple_of(t * BQ, BQ)
            q_blk = mixed_ref[pl.ds(qs, BQ), qcol : qcol + HD]
            g_blk = mixed_ref[pl.ds(qs, BQ), gcol : gcol + HD]
            lo = lo_ref[:, pl.ds(qs, BQ)]
            kt_lo = bounds_ref[t]
            kt_mid = bounds_ref[tiles + t]
            kt_hi = rim_tiles + t

            def allowed_at(kt):
                k_pos = kt * BK + lax.broadcasted_iota(jnp.int32, (BK, BQ), 0)
                q_pos = group + qs + lax.broadcasted_iota(jnp.int32, (BK, BQ), 1)
                return (k_pos >= lo) & (k_pos <= q_pos)

            def sweep(step):
                def masked(kt, c):
                    step(kt, True)
                    return c

                def interior(kt, c):
                    step(kt, False)
                    return c

                lax.fori_loop(kt_lo, kt_mid, masked, 0)
                lax.fori_loop(kt_mid, kt_hi, interior, 0)
                step(kt_hi, True)

            def forward_step(kt, masked):
                row = pl.multiple_of(kt * BK, BK)
                s = dot_t(kv_ref[pl.ds(row, BK), 0:HD], q_blk) * scale
                if masked:
                    s = jnp.where(allowed_at(kt), s, NEG)
                dp = dot_t(kv_ref[pl.ds(row, BK), HD : 2 * HD], g_blk)
                m_old = m_scr[...]
                m_new = jnp.maximum(m_old, jnp.max(s, axis=0, keepdims=True))
                alpha = jnp.exp(m_old - m_new)
                p = jnp.exp(s - m_new)
                l_scr[...] = alpha * l_scr[...] + jnp.sum(p, axis=0, keepdims=True)
                dl_scr[...] = alpha * dl_scr[...] + jnp.sum(p * dp, axis=0, keepdims=True)
                m_scr[...] = m_new

            m_scr[...] = jnp.full(m_scr.shape, NEG, jnp.float32)
            l_scr[...] = jnp.zeros(l_scr.shape, jnp.float32)
            dl_scr[...] = jnp.zeros(dl_scr.shape, jnp.float32)
            sweep(forward_step)
            inv_l = 1.0 / l_scr[...]
            l_scr[...] = inv_l
            dl_scr[...] = dl_scr[...] * inv_l
            dq_acc[...] = jnp.zeros(dq_acc.shape, jnp.float32)

            def backward_step(kt, masked):
                row = pl.multiple_of(kt * BK, BK)
                s = dot_t(kv_ref[pl.ds(row, BK), 0:HD], q_blk) * scale
                prob = jnp.exp(s - m_scr[...]) * l_scr[...]
                if masked:
                    prob = jnp.where(allowed_at(kt), prob, 0.0)
                dp = dot_t(kv_ref[pl.ds(row, BK), HD : 2 * HD], g_blk)
                ds = (prob * (dp - dl_scr[...]) * scale).astype(jnp.bfloat16)
                dk_ref[pl.ds(row, BK), :] += jnp.dot(ds, q_blk, preferred_element_type=jnp.float32)
                dv_ref[pl.ds(row, BK), :] += jnp.dot(
                    prob.astype(jnp.bfloat16), g_blk, preferred_element_type=jnp.float32
                )
                dq_acc[...] += jnp.dot(
                    kt_ref[:, pl.ds(row, BK)], ds, preferred_element_type=jnp.float32
                )

            sweep(backward_step)
            dq_ref[pl.ds(qs, BQ), qcol : qcol + HD] = dq_acc[...].T.astype(dq_ref.dtype)
            return carry

        lax.fori_loop(0, tiles, query_tile, 0)


def attend(bounds, mixed, kv, kt, lo, heads, interpret=False):
    group = mixed.shape[0]
    vmem = pltpu.MemorySpace.VMEM
    return pl.pallas_call(
        attend_kernel,
        out_shape=(
            jax.ShapeDtypeStruct((group, heads * HD), jnp.bfloat16),
            jax.ShapeDtypeStruct((2 * group, HD), jnp.float32),
            jax.ShapeDtypeStruct((2 * group, HD), jnp.float32),
        ),
        in_specs=[pl.BlockSpec(memory_space=pltpu.SMEM)]
        + [pl.BlockSpec(memory_space=vmem) for _ in range(4)],
        out_specs=tuple(pl.BlockSpec(memory_space=vmem) for _ in range(3)),
        scratch_shapes=[
            pltpu.VMEM((HD, BQ), jnp.float32),
            pltpu.VMEM((1, BQ), jnp.float32),
            pltpu.VMEM((1, BQ), jnp.float32),
            pltpu.VMEM((1, BQ), jnp.float32),
        ],
        compiler_params=pltpu.CompilerParams(vmem_limit_bytes=48 * 1024 * 1024),
        interpret=interpret,
    )(bounds, mixed, kv, kt, lo)


def key_bounds(lo, group):
    tiles = group // BQ
    kt_lo = lo[::BQ] // BK
    kt_hi = group // BK + jnp.arange(tiles, dtype=jnp.int32)
    kt_mid = jnp.clip((lo[BQ - 1 :: BQ] + BK - 1) // BK, kt_lo, kt_hi)
    return jnp.concatenate([kt_lo, kt_mid]).astype(jnp.int32)


def doc_starts(doc_lengths, positions):
    ends = jnp.cumsum(doc_lengths)
    starts = ends - doc_lengths
    return jnp.max(jnp.where(starts[None, :] <= positions[:, None], starts[None, :], 0), axis=1)


def body(queries, key_states, value_states, grad_out, doc_lengths):
    seq_count = lax.axis_size("seq")
    repeat = max(1, seq_count // KVH)
    rows = queries.shape[0]
    packed = jnp.concatenate(
        [
            queries.reshape(rows, seq_count, -1),
            grad_out.reshape(rows, seq_count, -1),
            expand_heads(key_states, repeat).reshape(rows, seq_count, -1),
            expand_heads(value_states, repeat).reshape(rows, seq_count, -1),
        ],
        axis=2,
    ).reshape(rows, -1)
    mixed = lax.all_to_all(packed, "seq", split_axis=1, concat_axis=0, tiled=True)
    group = mixed.shape[0]
    heads = queries.shape[1] // (seq_count * HD)
    kcol = 2 * heads * HD
    rim = from_behind(mixed[:, kcol : kcol + 2 * HD], "dp", 1)
    kv = jnp.concatenate([rim, mixed[:, kcol : kcol + 2 * HD]], axis=0)
    keys_t = kv[:, :HD].T
    root = lax.axis_index("dp") * group
    positions = root + jnp.arange(group, dtype=jnp.int32)
    lo = (doc_starts(doc_lengths, positions) - root + group).astype(jnp.int32)
    dq, dk, dv = attend(key_bounds(lo, group), mixed, kv, keys_t, lo.reshape(1, group), heads)
    rim_grad = jnp.concatenate([dk[:group], dv[:group]], axis=1).astype(jnp.bfloat16)
    back = from_behind(rim_grad, "dp", -1).astype(jnp.float32)
    own = (jnp.concatenate([dk[group:], dv[group:]], axis=1) + back).astype(jnp.bfloat16)
    out_packed = jnp.concatenate([dq, own], axis=1)
    returned = lax.all_to_all(out_packed, "seq", split_axis=0, concat_axis=1, tiled=True)
    returned = returned.reshape(rows, seq_count, -1)
    qw = heads * HD
    grad_queries = returned[:, :, :qw].reshape(rows, seq_count * qw)

    def fold(part):
        total = jnp.sum(part.astype(jnp.float32).reshape(rows, KVH, repeat, HD), axis=2)
        return total.reshape(rows, KVH * HD).astype(jnp.bfloat16)

    grad_keys = fold(returned[:, :, qw : qw + HD])
    grad_values = fold(returned[:, :, qw + HD : qw + 2 * HD])
    return (grad_queries, grad_keys, grad_values)


def solution(mesh):
    return jax.shard_map(
        body,
        mesh=mesh,
        in_specs=(
            P(("dp", "seq"), None),
            P(("dp", "seq"), None),
            P(("dp", "seq"), None),
            P(("dp", "seq"), None),
            P(),
        ),
        out_specs=(P(("dp", "seq"), None), P(("dp", "seq"), None), P(("dp", "seq"), None)),
        check_vma=False,
    )
```

```python
import jax
import jax.numpy as jnp
from jax import lax
from jax.experimental import pallas as pl
from jax.experimental.pallas import tpu as pltpu
from jax.sharding import PartitionSpec as P

KVH = 4
HD = 128
BQ = 512
BK = 512
NEG = -1e30


def from_behind(value, axis, steps):
    count = lax.axis_size(axis)
    initial, last = (max(0, -steps), min(count, count - steps))
    return lax.ppermute(value, axis, [(source, source + steps) for source in range(initial, last)])


def expand_heads(states, repeat):
    rows = states.shape[0]
    grouped = states.reshape(rows, KVH, HD)
    return jnp.repeat(grouped, repeat, axis=1).reshape(rows, KVH * repeat * HD)


def dot_t(a, b):
    return lax.dot_general(a, b, (((1,), (1,)), ((), ())), preferred_element_type=jnp.float32)


def attend_kernel(
    meta_ref, mixed_ref, rim_ref, dq_ref, rim_out, own_out,
    kv_scr, kt_scr, lo_scr, dk_acc, dv_acc, dq_acc, m_scr, l_scr, dl_scr,
):
    group = mixed_ref.shape[0]
    heads = dq_ref.shape[1] // HD
    tiles = group // BQ
    rim_tiles = group // BK
    docs = meta_ref.shape[0] - 1
    scale = HD ** (-0.5)
    kcol = 2 * heads * HD
    root = meta_ref[0]

    kv_scr[0:group, :] = rim_ref[...]
    kv_scr[group : 2 * group, :] = mixed_ref[:, kcol : kcol + 2 * HD]
    for c in range(2 * group // BK):
        kt_scr[:, c * BK : (c + 1) * BK] = (
            kv_scr[c * BK : (c + 1) * BK, 0:HD].astype(jnp.float32).T.astype(jnp.bfloat16)
        )
    dk_acc[...] = jnp.zeros(dk_acc.shape, jnp.float32)
    dv_acc[...] = jnp.zeros(dv_acc.shape, jnp.float32)

    positions = root + lax.broadcasted_iota(jnp.int32, (1, group), 1)

    def start_of(d, carry):
        begin, lo = carry
        lo = jnp.where(begin <= positions, begin, lo)
        return begin + meta_ref[d + 1], lo

    _, lo_vec = lax.fori_loop(0, docs, start_of, (jnp.int32(0), jnp.zeros((1, group), jnp.int32)))
    lo_scr[...] = lo_vec - root + group

    def doc_start(position):
        def step(d, carry):
            begin, found = carry
            found = jnp.where(begin <= position, begin, found)
            return begin + meta_ref[d + 1], found

        return lax.fori_loop(0, docs, step, (jnp.int32(0), jnp.int32(0)))[1] - root + group

    for h in range(heads):
        qcol = h * HD
        gcol = heads * HD + h * HD

        def query_tile(t, carry, qcol=qcol, gcol=gcol):
            qs = pl.multiple_of(t * BQ, BQ)
            q_blk = mixed_ref[pl.ds(qs, BQ), qcol : qcol + HD]
            g_blk = mixed_ref[pl.ds(qs, BQ), gcol : gcol + HD]
            lo = lo_scr[:, pl.ds(qs, BQ)]
            kt_hi = rim_tiles + t
            kt_lo = doc_start(root + qs) // BK
            kt_mid = jnp.minimum(jnp.maximum((doc_start(root + qs + BQ - 1) + BK - 1) // BK, kt_lo), kt_hi)

            def allowed_at(kt):
                k_pos = kt * BK + lax.broadcasted_iota(jnp.int32, (BK, BQ), 0)
                q_pos = group + qs + lax.broadcasted_iota(jnp.int32, (BK, BQ), 1)
                return (k_pos >= lo) & (k_pos <= q_pos)

            def sweep(step):
                def masked(kt, c):
                    step(kt, True)
                    return c

                def interior(kt, c):
                    step(kt, False)
                    return c

                lax.fori_loop(kt_lo, kt_mid, masked, 0)
                lax.fori_loop(kt_mid, kt_hi, interior, 0)
                step(kt_hi, True)

            def forward_step(kt, masked):
                row = pl.multiple_of(kt * BK, BK)
                s = dot_t(kv_scr[pl.ds(row, BK), 0:HD], q_blk) * scale
                if masked:
                    s = jnp.where(allowed_at(kt), s, NEG)
                dp = dot_t(kv_scr[pl.ds(row, BK), HD : 2 * HD], g_blk)
                m_old = m_scr[...]
                m_new = jnp.maximum(m_old, jnp.max(s, axis=0, keepdims=True))
                alpha = jnp.exp(m_old - m_new)
                p = jnp.exp(s - m_new)
                l_scr[...] = alpha * l_scr[...] + jnp.sum(p, axis=0, keepdims=True)
                dl_scr[...] = alpha * dl_scr[...] + jnp.sum(p * dp, axis=0, keepdims=True)
                m_scr[...] = m_new

            m_scr[...] = jnp.full(m_scr.shape, NEG, jnp.float32)
            l_scr[...] = jnp.zeros(l_scr.shape, jnp.float32)
            dl_scr[...] = jnp.zeros(dl_scr.shape, jnp.float32)
            sweep(forward_step)
            inv_l = 1.0 / l_scr[...]
            l_scr[...] = inv_l
            dl_scr[...] = dl_scr[...] * inv_l
            dq_acc[...] = jnp.zeros(dq_acc.shape, jnp.float32)

            def backward_step(kt, masked):
                row = pl.multiple_of(kt * BK, BK)
                s = dot_t(kv_scr[pl.ds(row, BK), 0:HD], q_blk) * scale
                prob = jnp.exp(s - m_scr[...]) * l_scr[...]
                if masked:
                    prob = jnp.where(allowed_at(kt), prob, 0.0)
                dp = dot_t(kv_scr[pl.ds(row, BK), HD : 2 * HD], g_blk)
                ds = (prob * (dp - dl_scr[...]) * scale).astype(jnp.bfloat16)
                dk_acc[pl.ds(row, BK), :] += jnp.dot(ds, q_blk, preferred_element_type=jnp.float32)
                dv_acc[pl.ds(row, BK), :] += jnp.dot(
                    prob.astype(jnp.bfloat16), g_blk, preferred_element_type=jnp.float32
                )
                dq_acc[...] += jnp.dot(
                    kt_scr[:, pl.ds(row, BK)], ds, preferred_element_type=jnp.float32
                )

            sweep(backward_step)
            dq_ref[pl.ds(qs, BQ), qcol : qcol + HD] = dq_acc[...].T.astype(dq_ref.dtype)
            return carry

        lax.fori_loop(0, tiles, query_tile, 0)

    rim_out[:, 0:HD] = dk_acc[0:group, :].astype(rim_out.dtype)
    rim_out[:, HD : 2 * HD] = dv_acc[0:group, :].astype(rim_out.dtype)
    own_out[:, 0:HD] = dk_acc[group : 2 * group, :]
    own_out[:, HD : 2 * HD] = dv_acc[group : 2 * group, :]


def attend(meta, mixed, rim, heads, interpret=False):
    group = mixed.shape[0]
    vmem = pltpu.MemorySpace.VMEM
    return pl.pallas_call(
        attend_kernel,
        out_shape=(
            jax.ShapeDtypeStruct((group, heads * HD), jnp.bfloat16),
            jax.ShapeDtypeStruct((group, 2 * HD), jnp.bfloat16),
            jax.ShapeDtypeStruct((group, 2 * HD), jnp.float32),
        ),
        in_specs=[pl.BlockSpec(memory_space=pltpu.SMEM)]
        + [pl.BlockSpec(memory_space=vmem) for _ in range(2)],
        out_specs=tuple(pl.BlockSpec(memory_space=vmem) for _ in range(3)),
        scratch_shapes=[
            pltpu.VMEM((2 * group, 2 * HD), jnp.bfloat16),
            pltpu.VMEM((HD, 2 * group), jnp.bfloat16),
            pltpu.VMEM((1, group), jnp.int32),
            pltpu.VMEM((2 * group, HD), jnp.float32),
            pltpu.VMEM((2 * group, HD), jnp.float32),
            pltpu.VMEM((HD, BQ), jnp.float32),
            pltpu.VMEM((1, BQ), jnp.float32),
            pltpu.VMEM((1, BQ), jnp.float32),
            pltpu.VMEM((1, BQ), jnp.float32),
        ],
        compiler_params=pltpu.CompilerParams(vmem_limit_bytes=48 * 1024 * 1024),
        interpret=interpret,
    )(meta, mixed, rim)


def body(queries, key_states, value_states, grad_out, doc_lengths):
    seq_count = lax.axis_size("seq")
    repeat = max(1, seq_count // KVH)
    rows = queries.shape[0]

    def by_destination(x):
        return x.reshape(rows, seq_count, -1).transpose(1, 0, 2)

    packed = jnp.concatenate(
        [
            by_destination(queries),
            by_destination(grad_out),
            by_destination(expand_heads(key_states, repeat)),
            by_destination(expand_heads(value_states, repeat)),
        ],
        axis=2,
    )
    mixed = lax.all_to_all(packed, "seq", split_axis=0, concat_axis=0, tiled=True)
    mixed = mixed.reshape(seq_count * rows, -1)
    group = mixed.shape[0]
    heads = queries.shape[1] // (seq_count * HD)
    kcol = 2 * heads * HD
    rim = from_behind(mixed[:, kcol : kcol + 2 * HD], "dp", 1)
    root = lax.axis_index("dp") * group
    meta = jnp.concatenate([root.reshape(1), doc_lengths]).astype(jnp.int32)
    dq, rim_grad, own = attend(meta, mixed, rim, heads)
    back = from_behind(rim_grad, "dp", -1).astype(jnp.float32)
    own = (own + back).astype(jnp.bfloat16)
    out_packed = jnp.concatenate([dq, own], axis=1).reshape(seq_count, rows, -1)
    returned = lax.all_to_all(out_packed, "seq", split_axis=0, concat_axis=0, tiled=True)
    qw = heads * HD
    grad_queries = returned[:, :, :qw].transpose(1, 0, 2).reshape(rows, seq_count * qw)

    def fold(part):
        part = part.astype(jnp.float32).reshape(KVH, repeat, rows, HD)
        return jnp.sum(part, axis=1).transpose(1, 0, 2).reshape(rows, KVH * HD).astype(jnp.bfloat16)

    grad_keys = fold(returned[:, :, qw : qw + HD])
    grad_values = fold(returned[:, :, qw + HD : qw + 2 * HD])
    return (grad_queries, grad_keys, grad_values)


def solution(mesh):
    return jax.shard_map(
        body,
        mesh=mesh,
        in_specs=(
            P(("dp", "seq"), None),
            P(("dp", "seq"), None),
            P(("dp", "seq"), None),
            P(("dp", "seq"), None),
            P(),
        ),
        out_specs=(P(("dp", "seq"), None), P(("dp", "seq"), None), P(("dp", "seq"), None)),
        check_vma=False,
    )
```

```python
import jax
import jax.numpy as jnp
from jax import lax
from jax.experimental import pallas as pl
from jax.experimental.pallas import tpu as pltpu
from jax.sharding import PartitionSpec as P

KVH = 4
HD = 128
BQ = 512
BK = 512
NEG = -1e30


def from_behind(value, axis, steps):
    count = lax.axis_size(axis)
    initial, last = (max(0, -steps), min(count, count - steps))
    return lax.ppermute(value, axis, [(source, source + steps) for source in range(initial, last)])


def expand_heads(states, repeat):
    rows = states.shape[0]
    grouped = states.reshape(rows, KVH, HD)
    return jnp.repeat(grouped, repeat, axis=1).reshape(rows, KVH * repeat * HD)


def dot_t(a, b):
    return lax.dot_general(a, b, (((1,), (1,)), ((), ())), preferred_element_type=jnp.float32)


def attend_kernel(
    meta_ref, mixed_ref, rim_ref, dq_ref, rim_out, own_out,
    kv_scr, kt_scr, lo_scr, dk_acc, dv_acc, dq_acc, m_scr, l_scr, dl_scr, s_scr, dp_scr,
):
    group = mixed_ref.shape[0]
    heads = dq_ref.shape[1] // HD
    tiles = group // BQ
    rim_tiles = group // BK
    docs = meta_ref.shape[0] - 1
    scale = HD ** (-0.5)
    kcol = 2 * heads * HD
    root = meta_ref[0]

    kv_scr[0:group, :] = rim_ref[...]
    kv_scr[group : 2 * group, :] = mixed_ref[:, kcol : kcol + 2 * HD]
    for c in range(2 * group // BK):
        kt_scr[:, c * BK : (c + 1) * BK] = (
            kv_scr[c * BK : (c + 1) * BK, 0:HD].astype(jnp.float32).T.astype(jnp.bfloat16)
        )
    dk_acc[...] = jnp.zeros(dk_acc.shape, jnp.float32)
    dv_acc[...] = jnp.zeros(dv_acc.shape, jnp.float32)

    positions = root + lax.broadcasted_iota(jnp.int32, (1, group), 1)

    def start_of(d, carry):
        begin, lo = carry
        lo = jnp.where(begin <= positions, begin, lo)
        return begin + meta_ref[d + 1], lo

    _, lo_vec = lax.fori_loop(0, docs, start_of, (jnp.int32(0), jnp.zeros((1, group), jnp.int32)))
    lo_scr[...] = lo_vec - root + group

    def doc_start(position):
        def step(d, carry):
            begin, found = carry
            found = jnp.where(begin <= position, begin, found)
            return begin + meta_ref[d + 1], found

        return lax.fori_loop(0, docs, step, (jnp.int32(0), jnp.int32(0)))[1] - root + group

    for h in range(heads):
        qcol = h * HD
        gcol = heads * HD + h * HD

        def query_tile(t, carry, qcol=qcol, gcol=gcol):
            qs = pl.multiple_of(t * BQ, BQ)
            q_blk = mixed_ref[pl.ds(qs, BQ), qcol : qcol + HD]
            g_blk = mixed_ref[pl.ds(qs, BQ), gcol : gcol + HD]
            lo = lo_scr[:, pl.ds(qs, BQ)]
            kt_hi = rim_tiles + t
            kt_lo = jnp.maximum(doc_start(root + qs) // BK, t)
            kt_mid = jnp.minimum(jnp.maximum((doc_start(root + qs + BQ - 1) + BK - 1) // BK, kt_lo), kt_hi)

            def allowed_at(kt):
                k_pos = kt * BK + lax.broadcasted_iota(jnp.int32, (BK, BQ), 0)
                q_pos = group + qs + lax.broadcasted_iota(jnp.int32, (BK, BQ), 1)
                return (k_pos >= lo) & (k_pos <= q_pos)

            def sweep(step):
                def masked(kt, c):
                    step(kt, True)
                    return c

                def interior(kt, c):
                    step(kt, False)
                    return c

                lax.fori_loop(kt_lo, kt_mid, masked, 0)
                lax.fori_loop(kt_mid, kt_hi, interior, 0)
                step(kt_hi, True)

            def forward_step(kt, masked):
                row = pl.multiple_of(kt * BK, BK)
                s = dot_t(kv_scr[pl.ds(row, BK), 0:HD], q_blk) * scale
                if masked:
                    s = jnp.where(allowed_at(kt), s, NEG)
                dp = dot_t(kv_scr[pl.ds(row, BK), HD : 2 * HD], g_blk)
                s_scr[kt - t] = s
                dp_scr[kt - t] = dp
                m_old = m_scr[...]
                m_new = jnp.maximum(m_old, jnp.max(s, axis=0, keepdims=True))
                alpha = jnp.exp(m_old - m_new)
                p = jnp.exp(s - m_new)
                l_scr[...] = alpha * l_scr[...] + jnp.sum(p, axis=0, keepdims=True)
                dl_scr[...] = alpha * dl_scr[...] + jnp.sum(p * dp, axis=0, keepdims=True)
                m_scr[...] = m_new

            m_scr[...] = jnp.full(m_scr.shape, NEG, jnp.float32)
            l_scr[...] = jnp.zeros(l_scr.shape, jnp.float32)
            dl_scr[...] = jnp.zeros(dl_scr.shape, jnp.float32)
            sweep(forward_step)
            inv_l = 1.0 / l_scr[...]
            l_scr[...] = inv_l
            dl_scr[...] = dl_scr[...] * inv_l
            dq_acc[...] = jnp.zeros(dq_acc.shape, jnp.float32)

            def backward_step(kt, masked):
                row = pl.multiple_of(kt * BK, BK)
                prob = jnp.exp(s_scr[kt - t] - m_scr[...]) * l_scr[...]
                dp = dp_scr[kt - t]
                ds = (prob * (dp - dl_scr[...]) * scale).astype(jnp.bfloat16)
                dk_acc[pl.ds(row, BK), :] += jnp.dot(ds, q_blk, preferred_element_type=jnp.float32)
                dv_acc[pl.ds(row, BK), :] += jnp.dot(
                    prob.astype(jnp.bfloat16), g_blk, preferred_element_type=jnp.float32
                )
                dq_acc[...] += jnp.dot(
                    kt_scr[:, pl.ds(row, BK)], ds, preferred_element_type=jnp.float32
                )

            sweep(backward_step)
            dq_ref[pl.ds(qs, BQ), qcol : qcol + HD] = dq_acc[...].T.astype(dq_ref.dtype)
            return carry

        lax.fori_loop(0, tiles, query_tile, 0)

    rim_out[:, 0:HD] = dk_acc[0:group, :].astype(rim_out.dtype)
    rim_out[:, HD : 2 * HD] = dv_acc[0:group, :].astype(rim_out.dtype)
    own_out[:, 0:HD] = dk_acc[group : 2 * group, :]
    own_out[:, HD : 2 * HD] = dv_acc[group : 2 * group, :]


def attend(meta, mixed, rim, heads, interpret=False):
    group = mixed.shape[0]
    vmem = pltpu.MemorySpace.VMEM
    return pl.pallas_call(
        attend_kernel,
        out_shape=(
            jax.ShapeDtypeStruct((group, heads * HD), jnp.bfloat16),
            jax.ShapeDtypeStruct((group, 2 * HD), jnp.bfloat16),
            jax.ShapeDtypeStruct((group, 2 * HD), jnp.float32),
        ),
        in_specs=[pl.BlockSpec(memory_space=pltpu.SMEM)]
        + [pl.BlockSpec(memory_space=vmem) for _ in range(2)],
        out_specs=tuple(pl.BlockSpec(memory_space=vmem) for _ in range(3)),
        scratch_shapes=[
            pltpu.VMEM((2 * group, 2 * HD), jnp.bfloat16),
            pltpu.VMEM((HD, 2 * group), jnp.bfloat16),
            pltpu.VMEM((1, group), jnp.int32),
            pltpu.VMEM((2 * group, HD), jnp.float32),
            pltpu.VMEM((2 * group, HD), jnp.float32),
            pltpu.VMEM((HD, BQ), jnp.float32),
            pltpu.VMEM((1, BQ), jnp.float32),
            pltpu.VMEM((1, BQ), jnp.float32),
            pltpu.VMEM((1, BQ), jnp.float32),
            pltpu.VMEM((group // BK + 1, BK, BQ), jnp.float32),
            pltpu.VMEM((group // BK + 1, BK, BQ), jnp.float32),
        ],
        compiler_params=pltpu.CompilerParams(vmem_limit_bytes=48 * 1024 * 1024),
        interpret=interpret,
    )(meta, mixed, rim)


def body(queries, key_states, value_states, grad_out, doc_lengths):
    seq_count = lax.axis_size("seq")
    repeat = max(1, seq_count // KVH)
    rows = queries.shape[0]

    def by_destination(x):
        return x.reshape(rows, seq_count, -1).transpose(1, 0, 2)

    packed = jnp.concatenate(
        [
            by_destination(queries),
            by_destination(grad_out),
            by_destination(expand_heads(key_states, repeat)),
            by_destination(expand_heads(value_states, repeat)),
        ],
        axis=2,
    )
    mixed = lax.all_to_all(packed, "seq", split_axis=0, concat_axis=0, tiled=True)
    mixed = mixed.reshape(seq_count * rows, -1)
    group = mixed.shape[0]
    heads = queries.shape[1] // (seq_count * HD)
    kcol = 2 * heads * HD
    rim = from_behind(mixed[:, kcol : kcol + 2 * HD], "dp", 1)
    root = lax.axis_index("dp") * group
    meta = jnp.concatenate([root.reshape(1), doc_lengths]).astype(jnp.int32)
    dq, rim_grad, own = attend(meta, mixed, rim, heads)
    back = from_behind(rim_grad, "dp", -1).astype(jnp.float32)
    own = (own + back).astype(jnp.bfloat16)
    out_packed = jnp.concatenate([dq, own], axis=1).reshape(seq_count, rows, -1)
    returned = lax.all_to_all(out_packed, "seq", split_axis=0, concat_axis=0, tiled=True)
    qw = heads * HD
    grad_queries = returned[:, :, :qw].transpose(1, 0, 2).reshape(rows, seq_count * qw)

    def fold(part):
        part = part.astype(jnp.float32).reshape(KVH, repeat, rows, HD)
        return jnp.sum(part, axis=1).transpose(1, 0, 2).reshape(rows, KVH * HD).astype(jnp.bfloat16)

    grad_keys = fold(returned[:, :, qw : qw + HD])
    grad_values = fold(returned[:, :, qw + HD : qw + 2 * HD])
    return (grad_queries, grad_keys, grad_values)


def solution(mesh):
    return jax.shard_map(
        body,
        mesh=mesh,
        in_specs=(
            P(("dp", "seq"), None),
            P(("dp", "seq"), None),
            P(("dp", "seq"), None),
            P(("dp", "seq"), None),
            P(),
        ),
        out_specs=(P(("dp", "seq"), None), P(("dp", "seq"), None), P(("dp", "seq"), None)),
        check_vma=False,
    )
```

```python
import functools

import jax
import jax.numpy as jnp
from jax import lax
from jax.experimental import pallas as pl
from jax.experimental.pallas import tpu as pltpu
from jax.sharding import PartitionSpec as P

KVH = 4
HD = 128
BQ = 512
BK = 512
NEG = -1e30


def from_behind(value, axis, steps):
    count = lax.axis_size(axis)
    initial, last = (max(0, -steps), min(count, count - steps))
    return lax.ppermute(value, axis, [(source, source + steps) for source in range(initial, last)])


def expand_heads(states, repeat):
    rows = states.shape[0]
    grouped = states.reshape(rows, KVH, HD)
    return jnp.repeat(grouped, repeat, axis=1).reshape(rows, KVH * repeat * HD)


def dot_t(a, b):
    return lax.dot_general(a, b, (((1,), (1,)), ((), ())), preferred_element_type=jnp.float32)


def attend_kernel(phase, *refs):
    if phase == "early":
        meta_ref, mixed_ref, dq_ref, acc_out = refs[:4]
        rim_ref = dq_in = acc_in = rim_out = None
        scratch = refs[4:]
    elif phase == "rim":
        meta_ref, mixed_ref, rim_ref, dq_in, acc_in, dq_ref, acc_out, rim_out = refs[:8]
        scratch = refs[8:]
    else:
        meta_ref, mixed_ref, dq_in, acc_in, dq_ref, acc_out = refs[:6]
        rim_ref = rim_out = None
        scratch = refs[6:]
    kv_scr, kt_scr, lo_scr, dk_acc, dv_acc, dq_acc, m_scr, l_scr, dl_scr, s_scr, dp_scr = scratch
    group = mixed_ref.shape[0]
    heads = dq_ref.shape[1] // HD
    tiles = group // BQ
    rim_tiles = group // BK
    docs = meta_ref.shape[0] - 1
    scale = HD ** (-0.5)
    kcol = 2 * heads * HD
    root = meta_ref[0]

    kv_scr[group : 2 * group, :] = mixed_ref[:, kcol : kcol + 2 * HD]
    first_chunk = rim_tiles
    if rim_ref is not None:
        kv_scr[0:group, :] = rim_ref[...]
        first_chunk = 0
        dk_acc[0:group, :] = jnp.zeros((group, HD), jnp.float32)
        dv_acc[0:group, :] = jnp.zeros((group, HD), jnp.float32)
    for c in range(first_chunk, 2 * group // BK):
        kt_scr[:, c * BK : (c + 1) * BK] = (
            kv_scr[c * BK : (c + 1) * BK, 0:HD].astype(jnp.float32).T.astype(jnp.bfloat16)
        )
    if acc_in is None:
        dk_acc[group : 2 * group, :] = jnp.zeros((group, HD), jnp.float32)
        dv_acc[group : 2 * group, :] = jnp.zeros((group, HD), jnp.float32)
    else:
        dk_acc[group : 2 * group, :] = acc_in[:, 0:HD]
        dv_acc[group : 2 * group, :] = acc_in[:, HD : 2 * HD]
        dq_ref[...] = dq_in[...]

    positions = root + lax.broadcasted_iota(jnp.int32, (1, group), 1)

    def start_of(d, carry):
        begin, lo = carry
        lo = jnp.where(begin <= positions, begin, lo)
        return begin + meta_ref[d + 1], lo

    _, lo_vec = lax.fori_loop(0, docs, start_of, (jnp.int32(0), jnp.zeros((1, group), jnp.int32)))
    lo_scr[...] = lo_vec - root + group

    def doc_start(position):
        def step(d, carry):
            begin, found = carry
            found = jnp.where(begin <= position, begin, found)
            return begin + meta_ref[d + 1], found

        return lax.fori_loop(0, docs, step, (jnp.int32(0), jnp.int32(0)))[1] - root + group

    def needs_rim(t, count):
        return count + (doc_start(root + t * BQ) < group).astype(jnp.int32)

    t_rim = lax.fori_loop(0, tiles, needs_rim, jnp.int32(0))
    t_mid = t_rim + (tiles - t_rim + 1) // 2
    t_first, t_last = {"early": (t_rim, t_mid), "rim": (0, t_rim), "late": (t_mid, tiles)}[phase]

    for h in range(heads):
        qcol = h * HD
        gcol = heads * HD + h * HD

        def query_tile(t, carry, qcol=qcol, gcol=gcol):
            qs = pl.multiple_of(t * BQ, BQ)
            q_blk = mixed_ref[pl.ds(qs, BQ), qcol : qcol + HD]
            g_blk = mixed_ref[pl.ds(qs, BQ), gcol : gcol + HD]
            lo = lo_scr[:, pl.ds(qs, BQ)]
            kt_hi = rim_tiles + t
            kt_lo = jnp.maximum(doc_start(root + qs) // BK, t)
            kt_mid = jnp.minimum(jnp.maximum((doc_start(root + qs + BQ - 1) + BK - 1) // BK, kt_lo), kt_hi)

            def allowed_at(kt):
                k_pos = kt * BK + lax.broadcasted_iota(jnp.int32, (BK, BQ), 0)
                q_pos = group + qs + lax.broadcasted_iota(jnp.int32, (BK, BQ), 1)
                return (k_pos >= lo) & (k_pos <= q_pos)

            def sweep(step):
                def masked(kt, c):
                    step(kt, True)
                    return c

                def interior(kt, c):
                    step(kt, False)
                    return c

                lax.fori_loop(kt_lo, kt_mid, masked, 0)
                lax.fori_loop(kt_mid, kt_hi, interior, 0)
                step(kt_hi, True)

            def forward_step(kt, masked):
                row = pl.multiple_of(kt * BK, BK)
                s = dot_t(kv_scr[pl.ds(row, BK), 0:HD], q_blk) * scale
                if masked:
                    s = jnp.where(allowed_at(kt), s, NEG)
                dp = dot_t(kv_scr[pl.ds(row, BK), HD : 2 * HD], g_blk)
                s_scr[kt - t] = s
                dp_scr[kt - t] = dp
                m_old = m_scr[...]
                m_new = jnp.maximum(m_old, jnp.max(s, axis=0, keepdims=True))
                alpha = jnp.exp(m_old - m_new)
                p = jnp.exp(s - m_new)
                l_scr[...] = alpha * l_scr[...] + jnp.sum(p, axis=0, keepdims=True)
                dl_scr[...] = alpha * dl_scr[...] + jnp.sum(p * dp, axis=0, keepdims=True)
                m_scr[...] = m_new

            m_scr[...] = jnp.full(m_scr.shape, NEG, jnp.float32)
            l_scr[...] = jnp.zeros(l_scr.shape, jnp.float32)
            dl_scr[...] = jnp.zeros(dl_scr.shape, jnp.float32)
            sweep(forward_step)
            inv_l = 1.0 / l_scr[...]
            l_scr[...] = inv_l
            dl_scr[...] = dl_scr[...] * inv_l
            dq_acc[...] = jnp.zeros(dq_acc.shape, jnp.float32)

            def backward_step(kt, masked):
                row = pl.multiple_of(kt * BK, BK)
                prob = jnp.exp(s_scr[kt - t] - m_scr[...]) * l_scr[...]
                dp = dp_scr[kt - t]
                ds = (prob * (dp - dl_scr[...]) * scale).astype(jnp.bfloat16)
                dk_acc[pl.ds(row, BK), :] += jnp.dot(ds, q_blk, preferred_element_type=jnp.float32)
                dv_acc[pl.ds(row, BK), :] += jnp.dot(
                    prob.astype(jnp.bfloat16), g_blk, preferred_element_type=jnp.float32
                )
                dq_acc[...] += jnp.dot(
                    kt_scr[:, pl.ds(row, BK)], ds, preferred_element_type=jnp.float32
                )

            sweep(backward_step)
            dq_ref[pl.ds(qs, BQ), qcol : qcol + HD] = dq_acc[...].T.astype(dq_ref.dtype)
            return carry

        lax.fori_loop(t_first, t_last, query_tile, 0)

    if rim_out is not None:
        rim_out[:, 0:HD] = dk_acc[0:group, :].astype(rim_out.dtype)
        rim_out[:, HD : 2 * HD] = dv_acc[0:group, :].astype(rim_out.dtype)
    acc_out[:, 0:HD] = dk_acc[group : 2 * group, :]
    acc_out[:, HD : 2 * HD] = dv_acc[group : 2 * group, :]


def attend(phase, meta, mixed, *rest, heads, interpret=False):
    group = mixed.shape[0]
    vmem = pltpu.MemorySpace.VMEM
    out_shape = [
        jax.ShapeDtypeStruct((group, heads * HD), jnp.bfloat16),
        jax.ShapeDtypeStruct((group, 2 * HD), jnp.float32),
    ]
    if phase == "rim":
        out_shape.append(jax.ShapeDtypeStruct((group, 2 * HD), jnp.bfloat16))
    return pl.pallas_call(
        functools.partial(attend_kernel, phase),
        out_shape=tuple(out_shape),
        in_specs=[pl.BlockSpec(memory_space=pltpu.SMEM)]
        + [pl.BlockSpec(memory_space=vmem) for _ in range(1 + len(rest))],
        out_specs=tuple(pl.BlockSpec(memory_space=vmem) for _ in out_shape),
        scratch_shapes=[
            pltpu.VMEM((2 * group, 2 * HD), jnp.bfloat16),
            pltpu.VMEM((HD, 2 * group), jnp.bfloat16),
            pltpu.VMEM((1, group), jnp.int32),
            pltpu.VMEM((2 * group, HD), jnp.float32),
            pltpu.VMEM((2 * group, HD), jnp.float32),
            pltpu.VMEM((HD, BQ), jnp.float32),
            pltpu.VMEM((1, BQ), jnp.float32),
            pltpu.VMEM((1, BQ), jnp.float32),
            pltpu.VMEM((1, BQ), jnp.float32),
            pltpu.VMEM((group // BK + 1, BK, BQ), jnp.float32),
            pltpu.VMEM((group // BK + 1, BK, BQ), jnp.float32),
        ],
        compiler_params=pltpu.CompilerParams(vmem_limit_bytes=48 * 1024 * 1024),
        interpret=interpret,
    )(meta, mixed, *rest)


def body(queries, key_states, value_states, grad_out, doc_lengths):
    seq_count = lax.axis_size("seq")
    repeat = max(1, seq_count // KVH)
    rows = queries.shape[0]

    def by_destination(x):
        return x.reshape(rows, seq_count, -1).transpose(1, 0, 2)

    packed = jnp.concatenate(
        [
            by_destination(queries),
            by_destination(grad_out),
            by_destination(expand_heads(key_states, repeat)),
            by_destination(expand_heads(value_states, repeat)),
        ],
        axis=2,
    )
    mixed = lax.all_to_all(packed, "seq", split_axis=0, concat_axis=0, tiled=True)
    mixed = mixed.reshape(seq_count * rows, -1)
    group = mixed.shape[0]
    heads = queries.shape[1] // (seq_count * HD)
    kcol = 2 * heads * HD
    rim = from_behind(mixed[:, kcol : kcol + 2 * HD], "dp", 1)
    root = lax.axis_index("dp") * group
    meta = jnp.concatenate([root.reshape(1), doc_lengths]).astype(jnp.int32)
    dq, acc = attend("early", meta, mixed, heads=heads)
    dq, acc, rim_grad = attend("rim", meta, mixed, rim, dq, acc, heads=heads)
    back = from_behind(rim_grad, "dp", -1).astype(jnp.float32)
    dq, own = attend("late", meta, mixed, dq, acc, heads=heads)
    own = (own + back).astype(jnp.bfloat16)
    out_packed = jnp.concatenate([dq, own], axis=1).reshape(seq_count, rows, -1)
    returned = lax.all_to_all(out_packed, "seq", split_axis=0, concat_axis=0, tiled=True)
    qw = heads * HD
    grad_queries = returned[:, :, :qw].transpose(1, 0, 2).reshape(rows, seq_count * qw)

    def fold(part):
        part = part.astype(jnp.float32).reshape(KVH, repeat, rows, HD)
        return jnp.sum(part, axis=1).transpose(1, 0, 2).reshape(rows, KVH * HD).astype(jnp.bfloat16)

    grad_keys = fold(returned[:, :, qw : qw + HD])
    grad_values = fold(returned[:, :, qw + HD : qw + 2 * HD])
    return (grad_queries, grad_keys, grad_values)


def solution(mesh):
    return jax.shard_map(
        body,
        mesh=mesh,
        in_specs=(
            P(("dp", "seq"), None),
            P(("dp", "seq"), None),
            P(("dp", "seq"), None),
            P(("dp", "seq"), None),
            P(),
        ),
        out_specs=(P(("dp", "seq"), None), P(("dp", "seq"), None), P(("dp", "seq"), None)),
        check_vma=False,
    )
```

```python
import functools
import math

import jax
import jax.numpy as jnp
from jax import lax
from jax.experimental import pallas as pl
from jax.experimental.pallas import tpu as pltpu
from jax.sharding import PartitionSpec as P

KVH = 4
HD = 128
BQ = 512
BK = 512
NEG = -1e30


def from_behind(value, axis, steps):
    count = lax.axis_size(axis)
    initial, last = (max(0, -steps), min(count, count - steps))
    return lax.ppermute(value, axis, [(source, source + steps) for source in range(initial, last)])


def expand_heads(states, repeat):
    rows = states.shape[0]
    grouped = states.reshape(rows, KVH, HD)
    return jnp.repeat(grouped, repeat, axis=1).reshape(rows, KVH * repeat * HD)


def dot_t(a, b):
    return lax.dot_general(a, b, (((1,), (1,)), ((), ())), preferred_element_type=jnp.float32)


def attend_kernel(phase, *refs):
    if phase == "early":
        meta_ref, mixed_ref, dq_ref, acc_out = refs[:4]
        rim_ref = dq_in = acc_in = rim_out = None
        scratch = refs[4:]
    elif phase == "rim":
        meta_ref, mixed_ref, rim_ref, dq_in, acc_in, dq_ref, acc_out, rim_out = refs[:8]
        scratch = refs[8:]
    else:
        meta_ref, mixed_ref, dq_in, acc_in, dq_ref, acc_out = refs[:6]
        rim_ref = rim_out = None
        scratch = refs[6:]
    kv_scr, kt_scr, lo_scr, dk_acc, dv_acc, dq_acc, m_scr, l_scr, dl_scr, s_scr, dp_scr = scratch
    group = mixed_ref.shape[0]
    heads = dq_ref.shape[1] // HD
    tiles = group // BQ
    rim_tiles = group // BK
    docs = meta_ref.shape[0] - 1
    scale = HD ** (-0.5)
    scale2 = scale * math.log2(math.e)
    kcol = 2 * heads * HD
    root = meta_ref[0]

    kv_scr[group : 2 * group, :] = mixed_ref[:, kcol : kcol + 2 * HD]
    first_chunk = rim_tiles
    if rim_ref is not None:
        kv_scr[0:group, :] = rim_ref[...]
        first_chunk = 0
        dk_acc[0:group, :] = jnp.zeros((group, HD), jnp.float32)
        dv_acc[0:group, :] = jnp.zeros((group, HD), jnp.float32)
    for c in range(first_chunk, 2 * group // BK):
        kt_scr[:, c * BK : (c + 1) * BK] = (
            kv_scr[c * BK : (c + 1) * BK, 0:HD].astype(jnp.float32).T.astype(jnp.bfloat16)
        )
    if acc_in is None:
        dk_acc[group : 2 * group, :] = jnp.zeros((group, HD), jnp.float32)
        dv_acc[group : 2 * group, :] = jnp.zeros((group, HD), jnp.float32)
    else:
        dk_acc[group : 2 * group, :] = acc_in[:, 0:HD]
        dv_acc[group : 2 * group, :] = acc_in[:, HD : 2 * HD]
        dq_ref[...] = dq_in[...]

    positions = root + lax.broadcasted_iota(jnp.int32, (1, group), 1)

    def start_of(d, carry):
        begin, lo = carry
        lo = jnp.where(begin <= positions, begin, lo)
        return begin + meta_ref[d + 1], lo

    _, lo_vec = lax.fori_loop(0, docs, start_of, (jnp.int32(0), jnp.zeros((1, group), jnp.int32)))
    lo_scr[...] = lo_vec - root + group

    def doc_start(position):
        def step(d, carry):
            begin, found = carry
            found = jnp.where(begin <= position, begin, found)
            return begin + meta_ref[d + 1], found

        return lax.fori_loop(0, docs, step, (jnp.int32(0), jnp.int32(0)))[1] - root + group

    def needs_rim(t, count):
        return count + (doc_start(root + t * BQ) < group).astype(jnp.int32)

    t_rim = lax.fori_loop(0, tiles, needs_rim, jnp.int32(0))
    t_mid = t_rim + (tiles - t_rim + 1) // 2
    t_first, t_last = {"early": (t_rim, t_mid), "rim": (0, t_rim), "late": (t_mid, tiles)}[phase]

    for h in range(heads):
        qcol = h * HD
        gcol = heads * HD + h * HD

        def query_tile(t, carry, qcol=qcol, gcol=gcol):
            qs = pl.multiple_of(t * BQ, BQ)
            q_blk = mixed_ref[pl.ds(qs, BQ), qcol : qcol + HD]
            g_blk = mixed_ref[pl.ds(qs, BQ), gcol : gcol + HD]
            lo = lo_scr[:, pl.ds(qs, BQ)]
            kt_hi = rim_tiles + t
            kt_lo = jnp.maximum(doc_start(root + qs) // BK, t)
            kt_mid = jnp.minimum(jnp.maximum((doc_start(root + qs + BQ - 1) + BK - 1) // BK, kt_lo), kt_hi)

            def allowed_at(kt, causal):
                k_pos = kt * BK + lax.broadcasted_iota(jnp.int32, (BK, BQ), 0)
                q_pos = group + qs + lax.broadcasted_iota(jnp.int32, (BK, BQ), 1)
                if not causal:
                    return k_pos >= lo
                return (k_pos >= lo) & (k_pos <= q_pos)

            def sweep(step):
                def masked(kt, c):
                    step(kt, "start")
                    return c

                def interior(kt, c):
                    step(kt, None)
                    return c

                lax.fori_loop(kt_lo, kt_mid, masked, 0)
                lax.fori_loop(kt_mid, kt_hi, interior, 0)
                step(kt_hi, "diagonal")

            def forward_step(kt, masked):
                row = pl.multiple_of(kt * BK, BK)
                s = dot_t(kv_scr[pl.ds(row, BK), 0:HD], q_blk) * scale2
                if masked is not None:
                    s = jnp.where(allowed_at(kt, masked == "diagonal"), s, NEG)
                dp = dot_t(kv_scr[pl.ds(row, BK), HD : 2 * HD], g_blk)
                s_scr[kt - t] = s
                dp_scr[kt - t] = dp
                m_old = m_scr[...]
                m_new = jnp.maximum(m_old, jnp.max(s, axis=0, keepdims=True))
                alpha = jnp.exp2(m_old - m_new)
                p = jnp.exp2(s - m_new)
                l_scr[...] = alpha * l_scr[...] + jnp.sum(p, axis=0, keepdims=True)
                dl_scr[...] = alpha * dl_scr[...] + jnp.sum(p * dp, axis=0, keepdims=True)
                m_scr[...] = m_new

            m_scr[...] = jnp.full(m_scr.shape, NEG, jnp.float32)
            l_scr[...] = jnp.zeros(l_scr.shape, jnp.float32)
            dl_scr[...] = jnp.zeros(dl_scr.shape, jnp.float32)
            sweep(forward_step)
            inv_l = 1.0 / l_scr[...]
            l_scr[...] = inv_l
            dl_scr[...] = dl_scr[...] * inv_l
            dq_acc[...] = jnp.zeros(dq_acc.shape, jnp.float32)

            def backward_step(kt, masked):
                row = pl.multiple_of(kt * BK, BK)
                prob = jnp.exp2(s_scr[kt - t] - m_scr[...]) * l_scr[...]
                dp = dp_scr[kt - t]
                ds = (prob * (dp - dl_scr[...]) * scale).astype(jnp.bfloat16)
                dk_acc[pl.ds(row, BK), :] += jnp.dot(ds, q_blk, preferred_element_type=jnp.float32)
                dv_acc[pl.ds(row, BK), :] += jnp.dot(
                    prob.astype(jnp.bfloat16), g_blk, preferred_element_type=jnp.float32
                )
                dq_acc[...] += jnp.dot(
                    kt_scr[:, pl.ds(row, BK)], ds, preferred_element_type=jnp.float32
                )

            sweep(backward_step)
            dq_ref[pl.ds(qs, BQ), qcol : qcol + HD] = dq_acc[...].T.astype(dq_ref.dtype)
            return carry

        lax.fori_loop(t_first, t_last, query_tile, 0)

    if rim_out is not None:
        rim_out[:, 0:HD] = dk_acc[0:group, :].astype(rim_out.dtype)
        rim_out[:, HD : 2 * HD] = dv_acc[0:group, :].astype(rim_out.dtype)
    acc_out[:, 0:HD] = dk_acc[group : 2 * group, :]
    acc_out[:, HD : 2 * HD] = dv_acc[group : 2 * group, :]


def attend(phase, meta, mixed, *rest, heads, interpret=False):
    group = mixed.shape[0]
    vmem = pltpu.MemorySpace.VMEM
    out_shape = [
        jax.ShapeDtypeStruct((group, heads * HD), jnp.bfloat16),
        jax.ShapeDtypeStruct((group, 2 * HD), jnp.float32),
    ]
    if phase == "rim":
        out_shape.append(jax.ShapeDtypeStruct((group, 2 * HD), jnp.bfloat16))
    return pl.pallas_call(
        functools.partial(attend_kernel, phase),
        out_shape=tuple(out_shape),
        in_specs=[pl.BlockSpec(memory_space=pltpu.SMEM)]
        + [pl.BlockSpec(memory_space=vmem) for _ in range(1 + len(rest))],
        out_specs=tuple(pl.BlockSpec(memory_space=vmem) for _ in out_shape),
        scratch_shapes=[
            pltpu.VMEM((2 * group, 2 * HD), jnp.bfloat16),
            pltpu.VMEM((HD, 2 * group), jnp.bfloat16),
            pltpu.VMEM((1, group), jnp.int32),
            pltpu.VMEM((2 * group, HD), jnp.float32),
            pltpu.VMEM((2 * group, HD), jnp.float32),
            pltpu.VMEM((HD, BQ), jnp.float32),
            pltpu.VMEM((1, BQ), jnp.float32),
            pltpu.VMEM((1, BQ), jnp.float32),
            pltpu.VMEM((1, BQ), jnp.float32),
            pltpu.VMEM((group // BK + 1, BK, BQ), jnp.float32),
            pltpu.VMEM((group // BK + 1, BK, BQ), jnp.float32),
        ],
        compiler_params=pltpu.CompilerParams(vmem_limit_bytes=48 * 1024 * 1024),
        interpret=interpret,
    )(meta, mixed, *rest)


def body(queries, key_states, value_states, grad_out, doc_lengths):
    seq_count = lax.axis_size("seq")
    repeat = max(1, seq_count // KVH)
    rows = queries.shape[0]

    def by_destination(x):
        return x.reshape(rows, seq_count, -1).transpose(1, 0, 2)

    packed = jnp.concatenate(
        [
            by_destination(queries),
            by_destination(grad_out),
            by_destination(expand_heads(key_states, repeat)),
            by_destination(expand_heads(value_states, repeat)),
        ],
        axis=2,
    )
    mixed = lax.all_to_all(packed, "seq", split_axis=0, concat_axis=0, tiled=True)
    mixed = mixed.reshape(seq_count * rows, -1)
    group = mixed.shape[0]
    heads = queries.shape[1] // (seq_count * HD)
    kcol = 2 * heads * HD
    rim = from_behind(mixed[:, kcol : kcol + 2 * HD], "dp", 1)
    root = lax.axis_index("dp") * group
    meta = jnp.concatenate([root.reshape(1), doc_lengths]).astype(jnp.int32)
    dq, acc = attend("early", meta, mixed, heads=heads)
    dq, acc, rim_grad = attend("rim", meta, mixed, rim, dq, acc, heads=heads)
    back = from_behind(rim_grad, "dp", -1).astype(jnp.float32)
    dq, own = attend("late", meta, mixed, dq, acc, heads=heads)
    own = (own + back).astype(jnp.bfloat16)
    out_packed = jnp.concatenate([dq, own], axis=1).reshape(seq_count, rows, -1)
    returned = lax.all_to_all(out_packed, "seq", split_axis=0, concat_axis=0, tiled=True)
    qw = heads * HD
    grad_queries = returned[:, :, :qw].transpose(1, 0, 2).reshape(rows, seq_count * qw)

    def fold(part):
        part = part.astype(jnp.float32).reshape(KVH, repeat, rows, HD)
        return jnp.sum(part, axis=1).transpose(1, 0, 2).reshape(rows, KVH * HD).astype(jnp.bfloat16)

    grad_keys = fold(returned[:, :, qw : qw + HD])
    grad_values = fold(returned[:, :, qw + HD : qw + 2 * HD])
    return (grad_queries, grad_keys, grad_values)


def solution(mesh):
    return jax.shard_map(
        body,
        mesh=mesh,
        in_specs=(
            P(("dp", "seq"), None),
            P(("dp", "seq"), None),
            P(("dp", "seq"), None),
            P(("dp", "seq"), None),
            P(),
        ),
        out_specs=(P(("dp", "seq"), None), P(("dp", "seq"), None), P(("dp", "seq"), None)),
        check_vma=False,
    )
```

```python
import functools
import math

import jax
import jax.numpy as jnp
from jax import lax
from jax.experimental import pallas as pl
from jax.experimental.pallas import tpu as pltpu
from jax.sharding import PartitionSpec as P

KVH = 4
HD = 128
BQ = 512
BK = 512
NEG = -1e30


def from_behind(value, axis, steps):
    count = lax.axis_size(axis)
    initial, last = (max(0, -steps), min(count, count - steps))
    return lax.ppermute(value, axis, [(source, source + steps) for source in range(initial, last)])


def expand_heads(states, repeat):
    rows = states.shape[0]
    grouped = states.reshape(rows, KVH, HD)
    return jnp.repeat(grouped, repeat, axis=1).reshape(rows, KVH * repeat * HD)


def dot_t(a, b):
    return lax.dot_general(a, b, (((1,), (1,)), ((), ())), preferred_element_type=jnp.float32)


def attend_kernel(phase, *refs):
    if phase == "early":
        meta_ref, mixed_ref, dq_ref, acc_out = refs[:4]
        rim_ref = dq_in = acc_in = rim_out = None
        scratch = refs[4:]
    elif phase == "rim":
        meta_ref, mixed_ref, rim_ref, dq_in, acc_in, dq_ref, acc_out, rim_out = refs[:8]
        scratch = refs[8:]
    else:
        meta_ref, mixed_ref, dq_in, acc_in, dq_ref, acc_out = refs[:6]
        rim_ref = rim_out = None
        scratch = refs[6:]
    kv_scr, kt_scr, lo_scr, dk_acc, dv_acc, dq_acc, m_scr, l_scr, dl_scr, s_scr, dp_scr = scratch
    group = mixed_ref.shape[0]
    heads = dq_ref.shape[1] // HD
    tiles = group // BQ
    rim_tiles = group // BK
    docs = meta_ref.shape[0] - 1
    scale = HD ** (-0.5)
    scale2 = scale * math.log2(math.e)
    kcol = 2 * heads * HD
    root = meta_ref[0]

    kv_scr[group : 2 * group, :] = mixed_ref[:, kcol : kcol + 2 * HD]
    first_chunk = rim_tiles
    if rim_ref is not None:
        kv_scr[0:group, :] = rim_ref[...]
        first_chunk = 0
        dk_acc[0:group, :] = jnp.zeros((group, HD), jnp.float32)
        dv_acc[0:group, :] = jnp.zeros((group, HD), jnp.float32)
    for c in range(first_chunk, 2 * group // BK):
        kt_scr[:, c * BK : (c + 1) * BK] = (
            kv_scr[c * BK : (c + 1) * BK, 0:HD].astype(jnp.float32).T.astype(jnp.bfloat16)
        )
    if acc_in is None:
        dk_acc[group : 2 * group, :] = jnp.zeros((group, HD), jnp.float32)
        dv_acc[group : 2 * group, :] = jnp.zeros((group, HD), jnp.float32)
    else:
        dk_acc[group : 2 * group, :] = acc_in[:, 0:HD]
        dv_acc[group : 2 * group, :] = acc_in[:, HD : 2 * HD]
        dq_ref[...] = dq_in[...]

    positions = root + lax.broadcasted_iota(jnp.int32, (1, group), 1)

    def start_of(d, carry):
        begin, lo = carry
        lo = jnp.where(begin <= positions, begin, lo)
        return begin + meta_ref[d + 1], lo

    _, lo_vec = lax.fori_loop(0, docs, start_of, (jnp.int32(0), jnp.zeros((1, group), jnp.int32)))
    lo_scr[...] = lo_vec - root + group

    def doc_start(position):
        def step(d, carry):
            begin, found = carry
            found = jnp.where(begin <= position, begin, found)
            return begin + meta_ref[d + 1], found

        return lax.fori_loop(0, docs, step, (jnp.int32(0), jnp.int32(0)))[1] - root + group

    def needs_rim(t, count):
        return count + (doc_start(root + t * BQ) < group).astype(jnp.int32)

    t_rim = lax.fori_loop(0, tiles, needs_rim, jnp.int32(0))
    t_mid = t_rim + (tiles - t_rim + 1) // 2
    t_first, t_last = {"early": (t_rim, t_mid), "rim": (0, t_rim), "late": (t_mid, tiles)}[phase]

    for h in range(heads):
        qcol = h * HD
        gcol = heads * HD + h * HD

        def query_tile(t, carry, qcol=qcol, gcol=gcol):
            qs = pl.multiple_of(t * BQ, BQ)
            q_blk = mixed_ref[pl.ds(qs, BQ), qcol : qcol + HD]
            g_blk = mixed_ref[pl.ds(qs, BQ), gcol : gcol + HD]
            lo = lo_scr[:, pl.ds(qs, BQ)]
            kt_hi = rim_tiles + t
            kt_lo = jnp.maximum(doc_start(root + qs) // BK, t)
            kt_mid = jnp.minimum(jnp.maximum((doc_start(root + qs + BQ - 1) + BK - 1) // BK, kt_lo), kt_hi)

            half = BK // 2

            def allowed_at(kt, causal, shape=(BK, BQ), k0=0, c0=0):
                k_pos = kt * BK + k0 + lax.broadcasted_iota(jnp.int32, shape, 0)
                lo_part = lo if c0 == 0 else lo[:, c0:]
                if not causal:
                    return k_pos >= lo_part
                q_pos = group + qs + c0 + lax.broadcasted_iota(jnp.int32, shape, 1)
                return (k_pos >= lo_part) & (k_pos <= q_pos)

            def sweep(step):
                def masked(kt, c):
                    step(kt, "start")
                    return c

                def interior(kt, c):
                    step(kt, None)
                    return c

                lax.fori_loop(kt_lo, kt_mid, masked, 0)
                lax.fori_loop(kt_mid, kt_hi, interior, 0)
                step(kt_hi, "diagonal")

            def stats_update(s, dp, c0):
                w = s.shape[1]
                m_old = m_scr[:, c0 : c0 + w]
                m_new = jnp.maximum(m_old, jnp.max(s, axis=0, keepdims=True))
                alpha = jnp.exp2(m_old - m_new)
                p = jnp.exp2(s - m_new)
                l_scr[:, c0 : c0 + w] = alpha * l_scr[:, c0 : c0 + w] + jnp.sum(p, axis=0, keepdims=True)
                dl_scr[:, c0 : c0 + w] = alpha * dl_scr[:, c0 : c0 + w] + jnp.sum(
                    p * dp, axis=0, keepdims=True
                )
                m_scr[:, c0 : c0 + w] = m_new

            def forward_step(kt, masked):
                row = pl.multiple_of(kt * BK, BK)
                slot = kt - t
                if masked == "diagonal":
                    upper = pl.multiple_of(row + half, half)
                    s = dot_t(kv_scr[pl.ds(row, half), 0:HD], q_blk) * scale2
                    s = jnp.where(allowed_at(kt, True, (half, BQ)), s, NEG)
                    dp = dot_t(kv_scr[pl.ds(row, half), HD : 2 * HD], g_blk)
                    s_scr[slot, 0:half, :] = s
                    dp_scr[slot, 0:half, :] = dp
                    stats_update(s, dp, 0)
                    s = dot_t(kv_scr[pl.ds(upper, half), 0:HD], q_blk[half:]) * scale2
                    s = jnp.where(allowed_at(kt, True, (half, half), half, half), s, NEG)
                    dp = dot_t(kv_scr[pl.ds(upper, half), HD : 2 * HD], g_blk[half:])
                    s_scr[slot, half:BK, half:BQ] = s
                    dp_scr[slot, half:BK, half:BQ] = dp
                    stats_update(s, dp, half)
                    return
                s = dot_t(kv_scr[pl.ds(row, BK), 0:HD], q_blk) * scale2
                if masked is not None:
                    s = jnp.where(allowed_at(kt, False), s, NEG)
                dp = dot_t(kv_scr[pl.ds(row, BK), HD : 2 * HD], g_blk)
                s_scr[slot] = s
                dp_scr[slot] = dp
                stats_update(s, dp, 0)

            m_scr[...] = jnp.full(m_scr.shape, NEG, jnp.float32)
            l_scr[...] = jnp.zeros(l_scr.shape, jnp.float32)
            dl_scr[...] = jnp.zeros(dl_scr.shape, jnp.float32)
            sweep(forward_step)
            inv_l = 1.0 / l_scr[...]
            l_scr[...] = inv_l
            dl_scr[...] = dl_scr[...] * inv_l
            dq_acc[...] = jnp.zeros(dq_acc.shape, jnp.float32)

            def grads(rows0, nrows, c0, s, dp):
                w = s.shape[1]
                prob = jnp.exp2(s - m_scr[:, c0 : c0 + w]) * l_scr[:, c0 : c0 + w]
                ds = (prob * (dp - dl_scr[:, c0 : c0 + w]) * scale).astype(jnp.bfloat16)
                q_part = q_blk if c0 == 0 else q_blk[c0:]
                g_part = g_blk if c0 == 0 else g_blk[c0:]
                dk_acc[pl.ds(rows0, nrows), :] += jnp.dot(ds, q_part, preferred_element_type=jnp.float32)
                dv_acc[pl.ds(rows0, nrows), :] += jnp.dot(
                    prob.astype(jnp.bfloat16), g_part, preferred_element_type=jnp.float32
                )
                dq_acc[:, c0 : c0 + w] += jnp.dot(
                    kt_scr[:, pl.ds(rows0, nrows)], ds, preferred_element_type=jnp.float32
                )

            def backward_step(kt, masked):
                row = pl.multiple_of(kt * BK, BK)
                slot = kt - t
                if masked == "diagonal":
                    upper = pl.multiple_of(row + half, half)
                    grads(row, half, 0, s_scr[slot, 0:half, :], dp_scr[slot, 0:half, :])
                    grads(upper, half, half, s_scr[slot, half:BK, half:BQ], dp_scr[slot, half:BK, half:BQ])
                    return
                grads(row, BK, 0, s_scr[slot], dp_scr[slot])

            sweep(backward_step)
            dq_ref[pl.ds(qs, BQ), qcol : qcol + HD] = dq_acc[...].T.astype(dq_ref.dtype)
            return carry

        lax.fori_loop(t_first, t_last, query_tile, 0)

    if rim_out is not None:
        rim_out[:, 0:HD] = dk_acc[0:group, :].astype(rim_out.dtype)
        rim_out[:, HD : 2 * HD] = dv_acc[0:group, :].astype(rim_out.dtype)
    acc_out[:, 0:HD] = dk_acc[group : 2 * group, :]
    acc_out[:, HD : 2 * HD] = dv_acc[group : 2 * group, :]


def attend(phase, meta, mixed, *rest, heads, interpret=False):
    group = mixed.shape[0]
    vmem = pltpu.MemorySpace.VMEM
    out_shape = [
        jax.ShapeDtypeStruct((group, heads * HD), jnp.bfloat16),
        jax.ShapeDtypeStruct((group, 2 * HD), jnp.float32),
    ]
    if phase == "rim":
        out_shape.append(jax.ShapeDtypeStruct((group, 2 * HD), jnp.bfloat16))
    return pl.pallas_call(
        functools.partial(attend_kernel, phase),
        out_shape=tuple(out_shape),
        in_specs=[pl.BlockSpec(memory_space=pltpu.SMEM)]
        + [pl.BlockSpec(memory_space=vmem) for _ in range(1 + len(rest))],
        out_specs=tuple(pl.BlockSpec(memory_space=vmem) for _ in out_shape),
        scratch_shapes=[
            pltpu.VMEM((2 * group, 2 * HD), jnp.bfloat16),
            pltpu.VMEM((HD, 2 * group), jnp.bfloat16),
            pltpu.VMEM((1, group), jnp.int32),
            pltpu.VMEM((2 * group, HD), jnp.float32),
            pltpu.VMEM((2 * group, HD), jnp.float32),
            pltpu.VMEM((HD, BQ), jnp.float32),
            pltpu.VMEM((1, BQ), jnp.float32),
            pltpu.VMEM((1, BQ), jnp.float32),
            pltpu.VMEM((1, BQ), jnp.float32),
            pltpu.VMEM((group // BK + 1, BK, BQ), jnp.float32),
            pltpu.VMEM((group // BK + 1, BK, BQ), jnp.float32),
        ],
        compiler_params=pltpu.CompilerParams(vmem_limit_bytes=48 * 1024 * 1024),
        interpret=interpret,
    )(meta, mixed, *rest)


def body(queries, key_states, value_states, grad_out, doc_lengths):
    seq_count = lax.axis_size("seq")
    repeat = max(1, seq_count // KVH)
    rows = queries.shape[0]

    def by_destination(x):
        return x.reshape(rows, seq_count, -1).transpose(1, 0, 2)

    packed = jnp.concatenate(
        [
            by_destination(queries),
            by_destination(grad_out),
            by_destination(expand_heads(key_states, repeat)),
            by_destination(expand_heads(value_states, repeat)),
        ],
        axis=2,
    )
    mixed = lax.all_to_all(packed, "seq", split_axis=0, concat_axis=0, tiled=True)
    mixed = mixed.reshape(seq_count * rows, -1)
    group = mixed.shape[0]
    heads = queries.shape[1] // (seq_count * HD)
    kcol = 2 * heads * HD
    rim = from_behind(mixed[:, kcol : kcol + 2 * HD], "dp", 1)
    root = lax.axis_index("dp") * group
    meta = jnp.concatenate([root.reshape(1), doc_lengths]).astype(jnp.int32)
    dq, acc = attend("early", meta, mixed, heads=heads)
    dq, acc, rim_grad = attend("rim", meta, mixed, rim, dq, acc, heads=heads)
    back = from_behind(rim_grad, "dp", -1).astype(jnp.float32)
    dq, own = attend("late", meta, mixed, dq, acc, heads=heads)
    own = (own + back).astype(jnp.bfloat16)
    out_packed = jnp.concatenate([dq, own], axis=1).reshape(seq_count, rows, -1)
    returned = lax.all_to_all(out_packed, "seq", split_axis=0, concat_axis=0, tiled=True)
    qw = heads * HD
    grad_queries = returned[:, :, :qw].transpose(1, 0, 2).reshape(rows, seq_count * qw)

    def fold(part):
        part = part.astype(jnp.float32).reshape(KVH, repeat, rows, HD)
        return jnp.sum(part, axis=1).transpose(1, 0, 2).reshape(rows, KVH * HD).astype(jnp.bfloat16)

    grad_keys = fold(returned[:, :, qw : qw + HD])
    grad_values = fold(returned[:, :, qw + HD : qw + 2 * HD])
    return (grad_queries, grad_keys, grad_values)


def solution(mesh):
    return jax.shard_map(
        body,
        mesh=mesh,
        in_specs=(
            P(("dp", "seq"), None),
            P(("dp", "seq"), None),
            P(("dp", "seq"), None),
            P(("dp", "seq"), None),
            P(),
        ),
        out_specs=(P(("dp", "seq"), None), P(("dp", "seq"), None), P(("dp", "seq"), None)),
        check_vma=False,
    )
```

```python
import functools
import math

import jax
import jax.numpy as jnp
from jax import lax
from jax.experimental import pallas as pl
from jax.experimental.pallas import tpu as pltpu
from jax.sharding import PartitionSpec as P

KVH = 4
HD = 128
BQ = 512
BK = 512
NEG = -1e30


def from_behind(value, axis, steps):
    count = lax.axis_size(axis)
    initial, last = (max(0, -steps), min(count, count - steps))
    return lax.ppermute(value, axis, [(source, source + steps) for source in range(initial, last)])


def expand_heads(states, repeat):
    rows = states.shape[0]
    grouped = states.reshape(rows, KVH, HD)
    return jnp.repeat(grouped, repeat, axis=1).reshape(rows, KVH * repeat * HD)


def dot_t(a, b):
    return lax.dot_general(a, b, (((1,), (1,)), ((), ())), preferred_element_type=jnp.float32)


def attend_kernel(phase, *refs):
    if phase == "early":
        meta_ref, mixed_ref, dq_ref, acc_out = refs[:4]
        rim_ref = dq_in = acc_in = rim_out = None
        scratch = refs[4:]
    elif phase == "rim":
        meta_ref, mixed_ref, rim_ref, dq_in, acc_in, dq_ref, acc_out, rim_out = refs[:8]
        scratch = refs[8:]
    else:
        meta_ref, mixed_ref, dq_in, acc_in, dq_ref, acc_out = refs[:6]
        rim_ref = rim_out = None
        scratch = refs[6:]
    kv_scr, kt_scr, lo_scr, dk_acc, dv_acc, dq_acc, m_scr, l_scr, dl_scr, s_scr, dp_scr = scratch
    group = mixed_ref.shape[0]
    heads = dq_ref.shape[1] // HD
    tiles = group // BQ
    rim_tiles = group // BK
    docs = meta_ref.shape[0] - 1
    scale = HD ** (-0.5)
    scale2 = scale * math.log2(math.e)
    kcol = 2 * heads * HD
    root = meta_ref[0]

    kv_scr[group : 2 * group, :] = mixed_ref[:, kcol : kcol + 2 * HD]
    first_chunk = rim_tiles
    if rim_ref is not None:
        kv_scr[0:group, :] = rim_ref[...]
        first_chunk = 0
        dk_acc[0:group, :] = jnp.zeros((group, HD), jnp.float32)
        dv_acc[0:group, :] = jnp.zeros((group, HD), jnp.float32)
    for c in range(first_chunk, 2 * group // BK):
        kt_scr[:, c * BK : (c + 1) * BK] = (
            kv_scr[c * BK : (c + 1) * BK, 0:HD].astype(jnp.float32).T.astype(jnp.bfloat16)
        )
    if acc_in is None:
        dk_acc[group : 2 * group, :] = jnp.zeros((group, HD), jnp.float32)
        dv_acc[group : 2 * group, :] = jnp.zeros((group, HD), jnp.float32)
    else:
        dk_acc[group : 2 * group, :] = acc_in[:, 0:HD]
        dv_acc[group : 2 * group, :] = acc_in[:, HD : 2 * HD]
        dq_ref[...] = dq_in[...]

    positions = root + lax.broadcasted_iota(jnp.int32, (1, group), 1)

    def start_of(d, carry):
        begin, lo = carry
        lo = jnp.where(begin <= positions, begin, lo)
        return begin + meta_ref[d + 1], lo

    _, lo_vec = lax.fori_loop(0, docs, start_of, (jnp.int32(0), jnp.zeros((1, group), jnp.int32)))
    lo_scr[...] = lo_vec - root + group

    def doc_start(position):
        def step(d, carry):
            begin, found = carry
            found = jnp.where(begin <= position, begin, found)
            return begin + meta_ref[d + 1], found

        return lax.fori_loop(0, docs, step, (jnp.int32(0), jnp.int32(0)))[1] - root + group

    def needs_rim(t, count):
        return count + (doc_start(root + t * BQ) < group).astype(jnp.int32)

    t_rim = lax.fori_loop(0, tiles, needs_rim, jnp.int32(0))
    t_mid = t_rim + (tiles - t_rim + 1) // 2
    t_first, t_last = {"early": (t_rim, t_mid), "rim": (0, t_rim), "late": (t_mid, tiles)}[phase]

    for h in range(heads):
        qcol = h * HD
        gcol = heads * HD + h * HD

        def query_tile(t, carry, qcol=qcol, gcol=gcol):
            qs = pl.multiple_of(t * BQ, BQ)
            q_blk = mixed_ref[pl.ds(qs, BQ), qcol : qcol + HD]
            g_blk = mixed_ref[pl.ds(qs, BQ), gcol : gcol + HD]
            lo = lo_scr[:, pl.ds(qs, BQ)]
            kt_hi = rim_tiles + t
            kt_lo = jnp.maximum(doc_start(root + qs) // BK, t)
            kt_mid = jnp.minimum(jnp.maximum((doc_start(root + qs + BQ - 1) + BK - 1) // BK, kt_lo), kt_hi)

            half = BK // 2
            hk_lo = jnp.maximum(doc_start(root + qs) // half, 2 * t)

            def allowed_at(kt, causal, shape=(BK, BQ), k0=0, c0=0):
                k_pos = kt * BK + k0 + lax.broadcasted_iota(jnp.int32, shape, 0)
                lo_part = lo if c0 == 0 else lo[:, c0:]
                if not causal:
                    return k_pos >= lo_part
                q_pos = group + qs + c0 + lax.broadcasted_iota(jnp.int32, shape, 1)
                return (k_pos >= lo_part) & (k_pos <= q_pos)

            def sweep(step):
                def masked(hk, c):
                    step(hk, "start")
                    return c

                def interior(kt, c):
                    step(kt, None)
                    return c

                lax.fori_loop(hk_lo, 2 * kt_mid, masked, 0)
                lax.fori_loop(kt_mid, kt_hi, interior, 0)
                step(kt_hi, "diagonal")

            def stats_update(s, dp, c0):
                w = s.shape[1]
                m_old = m_scr[:, c0 : c0 + w]
                m_new = jnp.maximum(m_old, jnp.max(s, axis=0, keepdims=True))
                alpha = jnp.exp2(m_old - m_new)
                p = jnp.exp2(s - m_new)
                l_scr[:, c0 : c0 + w] = alpha * l_scr[:, c0 : c0 + w] + jnp.sum(p, axis=0, keepdims=True)
                dl_scr[:, c0 : c0 + w] = alpha * dl_scr[:, c0 : c0 + w] + jnp.sum(
                    p * dp, axis=0, keepdims=True
                )
                m_scr[:, c0 : c0 + w] = m_new

            def forward_step(kt, masked):
                row = pl.multiple_of(kt * BK, BK)
                slot = kt - t
                if masked == "diagonal":
                    upper = pl.multiple_of(row + half, half)
                    s = dot_t(kv_scr[pl.ds(row, half), 0:HD], q_blk) * scale2
                    s = jnp.where(allowed_at(kt, True, (half, BQ)), s, NEG)
                    dp = dot_t(kv_scr[pl.ds(row, half), HD : 2 * HD], g_blk)
                    s_scr[slot, 0:half, :] = s
                    dp_scr[slot, 0:half, :] = dp
                    stats_update(s, dp, 0)
                    s = dot_t(kv_scr[pl.ds(upper, half), 0:HD], q_blk[half:]) * scale2
                    s = jnp.where(allowed_at(kt, True, (half, half), half, half), s, NEG)
                    dp = dot_t(kv_scr[pl.ds(upper, half), HD : 2 * HD], g_blk[half:])
                    s_scr[slot, half:BK, half:BQ] = s
                    dp_scr[slot, half:BK, half:BQ] = dp
                    stats_update(s, dp, half)
                    return
                if masked == "start":
                    hrow = pl.multiple_of(kt * half, half)
                    slot = kt // 2 - t
                    off = pl.multiple_of((kt % 2) * half, half)
                    s = dot_t(kv_scr[pl.ds(hrow, half), 0:HD], q_blk) * scale2
                    k_pos = hrow + lax.broadcasted_iota(jnp.int32, (half, BQ), 0)
                    s = jnp.where(k_pos >= lo, s, NEG)
                    dp = dot_t(kv_scr[pl.ds(hrow, half), HD : 2 * HD], g_blk)
                    s_scr[slot, pl.ds(off, half), :] = s
                    dp_scr[slot, pl.ds(off, half), :] = dp
                    stats_update(s, dp, 0)
                    return
                s = dot_t(kv_scr[pl.ds(row, BK), 0:HD], q_blk) * scale2
                dp = dot_t(kv_scr[pl.ds(row, BK), HD : 2 * HD], g_blk)
                s_scr[slot] = s
                dp_scr[slot] = dp
                stats_update(s, dp, 0)

            m_scr[...] = jnp.full(m_scr.shape, NEG, jnp.float32)
            l_scr[...] = jnp.zeros(l_scr.shape, jnp.float32)
            dl_scr[...] = jnp.zeros(dl_scr.shape, jnp.float32)
            sweep(forward_step)
            inv_l = 1.0 / l_scr[...]
            l_scr[...] = inv_l
            dl_scr[...] = dl_scr[...] * inv_l
            dq_acc[...] = jnp.zeros(dq_acc.shape, jnp.float32)

            def grads(rows0, nrows, c0, s, dp):
                w = s.shape[1]
                prob = jnp.exp2(s - m_scr[:, c0 : c0 + w]) * l_scr[:, c0 : c0 + w]
                ds = (prob * (dp - dl_scr[:, c0 : c0 + w]) * scale).astype(jnp.bfloat16)
                q_part = q_blk if c0 == 0 else q_blk[c0:]
                g_part = g_blk if c0 == 0 else g_blk[c0:]
                dk_acc[pl.ds(rows0, nrows), :] += jnp.dot(ds, q_part, preferred_element_type=jnp.float32)
                dv_acc[pl.ds(rows0, nrows), :] += jnp.dot(
                    prob.astype(jnp.bfloat16), g_part, preferred_element_type=jnp.float32
                )
                dq_acc[:, c0 : c0 + w] += jnp.dot(
                    kt_scr[:, pl.ds(rows0, nrows)], ds, preferred_element_type=jnp.float32
                )

            def backward_step(kt, masked):
                row = pl.multiple_of(kt * BK, BK)
                slot = kt - t
                if masked == "diagonal":
                    upper = pl.multiple_of(row + half, half)
                    grads(row, half, 0, s_scr[slot, 0:half, :], dp_scr[slot, 0:half, :])
                    grads(upper, half, half, s_scr[slot, half:BK, half:BQ], dp_scr[slot, half:BK, half:BQ])
                    return
                if masked == "start":
                    hrow = pl.multiple_of(kt * half, half)
                    slot = kt // 2 - t
                    off = pl.multiple_of((kt % 2) * half, half)
                    grads(hrow, half, 0, s_scr[slot, pl.ds(off, half), :], dp_scr[slot, pl.ds(off, half), :])
                    return
                grads(row, BK, 0, s_scr[slot], dp_scr[slot])

            sweep(backward_step)
            dq_ref[pl.ds(qs, BQ), qcol : qcol + HD] = dq_acc[...].T.astype(dq_ref.dtype)
            return carry

        lax.fori_loop(t_first, t_last, query_tile, 0)

    if rim_out is not None:
        rim_out[:, 0:HD] = dk_acc[0:group, :].astype(rim_out.dtype)
        rim_out[:, HD : 2 * HD] = dv_acc[0:group, :].astype(rim_out.dtype)
    acc_out[:, 0:HD] = dk_acc[group : 2 * group, :]
    acc_out[:, HD : 2 * HD] = dv_acc[group : 2 * group, :]


def attend(phase, meta, mixed, *rest, heads, interpret=False):
    group = mixed.shape[0]
    vmem = pltpu.MemorySpace.VMEM
    out_shape = [
        jax.ShapeDtypeStruct((group, heads * HD), jnp.bfloat16),
        jax.ShapeDtypeStruct((group, 2 * HD), jnp.float32),
    ]
    if phase == "rim":
        out_shape.append(jax.ShapeDtypeStruct((group, 2 * HD), jnp.bfloat16))
    return pl.pallas_call(
        functools.partial(attend_kernel, phase),
        out_shape=tuple(out_shape),
        in_specs=[pl.BlockSpec(memory_space=pltpu.SMEM)]
        + [pl.BlockSpec(memory_space=vmem) for _ in range(1 + len(rest))],
        out_specs=tuple(pl.BlockSpec(memory_space=vmem) for _ in out_shape),
        scratch_shapes=[
            pltpu.VMEM((2 * group, 2 * HD), jnp.bfloat16),
            pltpu.VMEM((HD, 2 * group), jnp.bfloat16),
            pltpu.VMEM((1, group), jnp.int32),
            pltpu.VMEM((2 * group, HD), jnp.float32),
            pltpu.VMEM((2 * group, HD), jnp.float32),
            pltpu.VMEM((HD, BQ), jnp.float32),
            pltpu.VMEM((1, BQ), jnp.float32),
            pltpu.VMEM((1, BQ), jnp.float32),
            pltpu.VMEM((1, BQ), jnp.float32),
            pltpu.VMEM((group // BK + 1, BK, BQ), jnp.float32),
            pltpu.VMEM((group // BK + 1, BK, BQ), jnp.float32),
        ],
        compiler_params=pltpu.CompilerParams(vmem_limit_bytes=48 * 1024 * 1024),
        interpret=interpret,
    )(meta, mixed, *rest)


def body(queries, key_states, value_states, grad_out, doc_lengths):
    seq_count = lax.axis_size("seq")
    repeat = max(1, seq_count // KVH)
    rows = queries.shape[0]

    def by_destination(x):
        return x.reshape(rows, seq_count, -1).transpose(1, 0, 2)

    packed = jnp.concatenate(
        [
            by_destination(queries),
            by_destination(grad_out),
            by_destination(expand_heads(key_states, repeat)),
            by_destination(expand_heads(value_states, repeat)),
        ],
        axis=2,
    )
    mixed = lax.all_to_all(packed, "seq", split_axis=0, concat_axis=0, tiled=True)
    mixed = mixed.reshape(seq_count * rows, -1)
    group = mixed.shape[0]
    heads = queries.shape[1] // (seq_count * HD)
    kcol = 2 * heads * HD
    rim = from_behind(mixed[:, kcol : kcol + 2 * HD], "dp", 1)
    root = lax.axis_index("dp") * group
    meta = jnp.concatenate([root.reshape(1), doc_lengths]).astype(jnp.int32)
    dq, acc = attend("early", meta, mixed, heads=heads)
    dq, acc, rim_grad = attend("rim", meta, mixed, rim, dq, acc, heads=heads)
    back = from_behind(rim_grad, "dp", -1).astype(jnp.float32)
    dq, own = attend("late", meta, mixed, dq, acc, heads=heads)
    own = (own + back).astype(jnp.bfloat16)
    out_packed = jnp.concatenate([dq, own], axis=1).reshape(seq_count, rows, -1)
    returned = lax.all_to_all(out_packed, "seq", split_axis=0, concat_axis=0, tiled=True)
    qw = heads * HD
    grad_queries = returned[:, :, :qw].transpose(1, 0, 2).reshape(rows, seq_count * qw)

    def fold(part):
        part = part.astype(jnp.float32).reshape(KVH, repeat, rows, HD)
        return jnp.sum(part, axis=1).transpose(1, 0, 2).reshape(rows, KVH * HD).astype(jnp.bfloat16)

    grad_keys = fold(returned[:, :, qw : qw + HD])
    grad_values = fold(returned[:, :, qw + HD : qw + 2 * HD])
    return (grad_queries, grad_keys, grad_values)


def solution(mesh):
    return jax.shard_map(
        body,
        mesh=mesh,
        in_specs=(
            P(("dp", "seq"), None),
            P(("dp", "seq"), None),
            P(("dp", "seq"), None),
            P(("dp", "seq"), None),
            P(),
        ),
        out_specs=(P(("dp", "seq"), None), P(("dp", "seq"), None), P(("dp", "seq"), None)),
        check_vma=False,
    )
```

```python
import functools
import math

import jax
import jax.numpy as jnp
from jax import lax
from jax.experimental import pallas as pl
from jax.experimental.pallas import tpu as pltpu
from jax.sharding import PartitionSpec as P

KVH = 4
HD = 128
BQ = 512
BK = 512
NEG = -1e30


def from_behind(value, axis, steps):
    count = lax.axis_size(axis)
    initial, last = (max(0, -steps), min(count, count - steps))
    return lax.ppermute(value, axis, [(source, source + steps) for source in range(initial, last)])


def expand_heads(states, repeat):
    rows = states.shape[0]
    grouped = states.reshape(rows, KVH, HD)
    return jnp.repeat(grouped, repeat, axis=1).reshape(rows, KVH * repeat * HD)


def dot_t(a, b):
    return lax.dot_general(a, b, (((1,), (1,)), ((), ())), preferred_element_type=jnp.float32)


def attend_kernel(phase, *refs):
    if phase == "early":
        meta_ref, mixed_ref, dq_ref, acc_out = refs[:4]
        rim_ref = dq_in = acc_in = rim_out = None
        scratch = refs[4:]
    elif phase == "rim":
        meta_ref, mixed_ref, rim_ref, dq_in, acc_in, dq_ref, acc_out, rim_out = refs[:8]
        scratch = refs[8:]
    else:
        meta_ref, mixed_ref, dq_in, acc_in, dq_ref, acc_out = refs[:6]
        rim_ref = rim_out = None
        scratch = refs[6:]
    kv_scr, kt_scr, lo_scr, dk_acc, dv_acc, dq_acc, m_scr, l_scr, dl_scr, s_scr, dp_scr = scratch
    group = mixed_ref.shape[0]
    heads = dq_ref.shape[1] // HD
    tiles = group // BQ
    rim_tiles = group // BK
    docs = meta_ref.shape[0] - 1
    scale = HD ** (-0.5)
    scale2 = scale * math.log2(math.e)
    kcol = 2 * heads * HD
    root = meta_ref[0]

    kv_scr[group : 2 * group, :] = mixed_ref[:, kcol : kcol + 2 * HD]
    first_chunk = rim_tiles
    if rim_ref is not None:
        kv_scr[0:group, :] = rim_ref[...]
        first_chunk = 0
        dk_acc[0:group, :] = jnp.zeros((group, HD), jnp.float32)
        dv_acc[0:group, :] = jnp.zeros((group, HD), jnp.float32)
    for c in range(first_chunk, 2 * group // BK):
        kt_scr[:, c * BK : (c + 1) * BK] = (
            kv_scr[c * BK : (c + 1) * BK, 0:HD].astype(jnp.float32).T.astype(jnp.bfloat16)
        )
    if acc_in is None:
        dk_acc[group : 2 * group, :] = jnp.zeros((group, HD), jnp.float32)
        dv_acc[group : 2 * group, :] = jnp.zeros((group, HD), jnp.float32)
    else:
        dk_acc[group : 2 * group, :] = acc_in[:, 0:HD]
        dv_acc[group : 2 * group, :] = acc_in[:, HD : 2 * HD]
        dq_ref[...] = dq_in[...]

    positions = root + lax.broadcasted_iota(jnp.int32, (1, group), 1)

    def start_of(d, carry):
        begin, lo = carry
        lo = jnp.where(begin <= positions, begin, lo)
        return begin + meta_ref[d + 1], lo

    _, lo_vec = lax.fori_loop(0, docs, start_of, (jnp.int32(0), jnp.zeros((1, group), jnp.int32)))
    lo_scr[...] = lo_vec - root + group

    def doc_start(position):
        def step(d, carry):
            begin, found = carry
            found = jnp.where(begin <= position, begin, found)
            return begin + meta_ref[d + 1], found

        return lax.fori_loop(0, docs, step, (jnp.int32(0), jnp.int32(0)))[1] - root + group

    def needs_rim(t, count):
        return count + (doc_start(root + t * BQ) < group).astype(jnp.int32)

    t_rim = lax.fori_loop(0, tiles, needs_rim, jnp.int32(0))
    t_mid = t_rim + (tiles - t_rim + 1) // 2
    t_first, t_last = {"early": (t_rim, t_mid), "rim": (0, t_rim), "late": (t_mid, tiles)}[phase]

    for h in range(heads):
        qcol = h * HD
        gcol = heads * HD + h * HD

        def query_tile(t, carry, qcol=qcol, gcol=gcol):
            qs = pl.multiple_of(t * BQ, BQ)
            q_blk = mixed_ref[pl.ds(qs, BQ), qcol : qcol + HD]
            g_blk = mixed_ref[pl.ds(qs, BQ), gcol : gcol + HD]
            lo = lo_scr[:, pl.ds(qs, BQ)]
            kt_hi = rim_tiles + t
            kt_lo = jnp.maximum(doc_start(root + qs) // BK, t)
            kt_mid = jnp.minimum(jnp.maximum((doc_start(root + qs + BQ - 1) + BK - 1) // BK, kt_lo), kt_hi)

            half = BK // 2

            def allowed_at(kt, causal, shape=(BK, BQ), k0=0, c0=0):
                k_pos = kt * BK + k0 + lax.broadcasted_iota(jnp.int32, shape, 0)
                lo_part = lo if c0 == 0 else lo[:, c0:]
                if not causal:
                    return k_pos >= lo_part
                q_pos = group + qs + c0 + lax.broadcasted_iota(jnp.int32, shape, 1)
                return (k_pos >= lo_part) & (k_pos <= q_pos)

            def sweep(step):
                def masked(kt, c):
                    step(kt, "start")
                    return c

                def interior(kt, c):
                    step(kt, None)
                    return c

                lax.fori_loop(kt_lo, kt_mid, masked, 0)
                lax.fori_loop(kt_mid, kt_hi, interior, 0)
                step(kt_hi, "diagonal")

            def stats_update(s, dp, c0):
                w = s.shape[1]
                m_old = m_scr[:, c0 : c0 + w]
                m_new = jnp.maximum(m_old, jnp.max(s, axis=0, keepdims=True))
                alpha = jnp.exp2(m_old - m_new)
                p = jnp.exp2(s - m_new)
                l_scr[:, c0 : c0 + w] = alpha * l_scr[:, c0 : c0 + w] + jnp.sum(p, axis=0, keepdims=True)
                dl_scr[:, c0 : c0 + w] = alpha * dl_scr[:, c0 : c0 + w] + jnp.sum(
                    p * dp, axis=0, keepdims=True
                )
                m_scr[:, c0 : c0 + w] = m_new

            def forward_step(kt, masked):
                row = pl.multiple_of(kt * BK, BK)
                slot = kt - t
                if masked == "diagonal":
                    upper = pl.multiple_of(row + half, half)
                    s = dot_t(kv_scr[pl.ds(row, half), 0:HD], q_blk) * scale2
                    s = jnp.where(allowed_at(kt, True, (half, BQ)), s, NEG)
                    dp = dot_t(kv_scr[pl.ds(row, half), HD : 2 * HD], g_blk)
                    s_scr[slot, 0:half, :] = s
                    dp_scr[slot, 0:half, :] = dp
                    stats_update(s, dp, 0)
                    s = dot_t(kv_scr[pl.ds(upper, half), 0:HD], q_blk[half:]) * scale2
                    s = jnp.where(allowed_at(kt, True, (half, half), half, half), s, NEG)
                    dp = dot_t(kv_scr[pl.ds(upper, half), HD : 2 * HD], g_blk[half:])
                    s_scr[slot, half:BK, half:BQ] = s
                    dp_scr[slot, half:BK, half:BQ] = dp
                    stats_update(s, dp, half)
                    return
                s = dot_t(kv_scr[pl.ds(row, BK), 0:HD], q_blk) * scale2
                if masked is not None:
                    s = jnp.where(allowed_at(kt, False), s, NEG)
                dp = dot_t(kv_scr[pl.ds(row, BK), HD : 2 * HD], g_blk)
                s_scr[slot] = s
                dp_scr[slot] = dp
                stats_update(s, dp, 0)

            m_scr[...] = jnp.full(m_scr.shape, NEG, jnp.float32)
            l_scr[...] = jnp.zeros(l_scr.shape, jnp.float32)
            dl_scr[...] = jnp.zeros(dl_scr.shape, jnp.float32)
            sweep(forward_step)
            inv_l = 1.0 / l_scr[...]
            m_scr[...] = m_scr[...] + jnp.log2(l_scr[...])
            dl_scr[...] = dl_scr[...] * inv_l
            dq_acc[...] = jnp.zeros(dq_acc.shape, jnp.float32)

            def grads(rows0, nrows, c0, s, dp):
                w = s.shape[1]
                prob = jnp.exp2(s - m_scr[:, c0 : c0 + w])
                ds = (prob * (dp - dl_scr[:, c0 : c0 + w]) * scale).astype(jnp.bfloat16)
                q_part = q_blk if c0 == 0 else q_blk[c0:]
                g_part = g_blk if c0 == 0 else g_blk[c0:]
                dk_acc[pl.ds(rows0, nrows), :] += jnp.dot(ds, q_part, preferred_element_type=jnp.float32)
                dv_acc[pl.ds(rows0, nrows), :] += jnp.dot(
                    prob.astype(jnp.bfloat16), g_part, preferred_element_type=jnp.float32
                )
                dq_acc[:, c0 : c0 + w] += jnp.dot(
                    kt_scr[:, pl.ds(rows0, nrows)], ds, preferred_element_type=jnp.float32
                )

            def backward_step(kt, masked):
                row = pl.multiple_of(kt * BK, BK)
                slot = kt - t
                if masked == "diagonal":
                    upper = pl.multiple_of(row + half, half)
                    grads(row, half, 0, s_scr[slot, 0:half, :], dp_scr[slot, 0:half, :])
                    grads(upper, half, half, s_scr[slot, half:BK, half:BQ], dp_scr[slot, half:BK, half:BQ])
                    return
                grads(row, BK, 0, s_scr[slot], dp_scr[slot])

            sweep(backward_step)
            dq_ref[pl.ds(qs, BQ), qcol : qcol + HD] = dq_acc[...].T.astype(dq_ref.dtype)
            return carry

        lax.fori_loop(t_first, t_last, query_tile, 0)

    if rim_out is not None:
        rim_out[:, 0:HD] = dk_acc[0:group, :].astype(rim_out.dtype)
        rim_out[:, HD : 2 * HD] = dv_acc[0:group, :].astype(rim_out.dtype)
    acc_out[:, 0:HD] = dk_acc[group : 2 * group, :]
    acc_out[:, HD : 2 * HD] = dv_acc[group : 2 * group, :]


def attend(phase, meta, mixed, *rest, heads, interpret=False):
    group = mixed.shape[0]
    vmem = pltpu.MemorySpace.VMEM
    out_shape = [
        jax.ShapeDtypeStruct((group, heads * HD), jnp.bfloat16),
        jax.ShapeDtypeStruct((group, 2 * HD), jnp.float32),
    ]
    if phase == "rim":
        out_shape.append(jax.ShapeDtypeStruct((group, 2 * HD), jnp.bfloat16))
    return pl.pallas_call(
        functools.partial(attend_kernel, phase),
        out_shape=tuple(out_shape),
        in_specs=[pl.BlockSpec(memory_space=pltpu.SMEM)]
        + [pl.BlockSpec(memory_space=vmem) for _ in range(1 + len(rest))],
        out_specs=tuple(pl.BlockSpec(memory_space=vmem) for _ in out_shape),
        scratch_shapes=[
            pltpu.VMEM((2 * group, 2 * HD), jnp.bfloat16),
            pltpu.VMEM((HD, 2 * group), jnp.bfloat16),
            pltpu.VMEM((1, group), jnp.int32),
            pltpu.VMEM((2 * group, HD), jnp.float32),
            pltpu.VMEM((2 * group, HD), jnp.float32),
            pltpu.VMEM((HD, BQ), jnp.float32),
            pltpu.VMEM((1, BQ), jnp.float32),
            pltpu.VMEM((1, BQ), jnp.float32),
            pltpu.VMEM((1, BQ), jnp.float32),
            pltpu.VMEM((group // BK + 1, BK, BQ), jnp.float32),
            pltpu.VMEM((group // BK + 1, BK, BQ), jnp.float32),
        ],
        compiler_params=pltpu.CompilerParams(vmem_limit_bytes=48 * 1024 * 1024),
        interpret=interpret,
    )(meta, mixed, *rest)


def body(queries, key_states, value_states, grad_out, doc_lengths):
    seq_count = lax.axis_size("seq")
    repeat = max(1, seq_count // KVH)
    rows = queries.shape[0]

    def by_destination(x):
        return x.reshape(rows, seq_count, -1).transpose(1, 0, 2)

    packed = jnp.concatenate(
        [
            by_destination(queries),
            by_destination(grad_out),
            by_destination(expand_heads(key_states, repeat)),
            by_destination(expand_heads(value_states, repeat)),
        ],
        axis=2,
    )
    mixed = lax.all_to_all(packed, "seq", split_axis=0, concat_axis=0, tiled=True)
    mixed = mixed.reshape(seq_count * rows, -1)
    group = mixed.shape[0]
    heads = queries.shape[1] // (seq_count * HD)
    kcol = 2 * heads * HD
    rim = from_behind(mixed[:, kcol : kcol + 2 * HD], "dp", 1)
    root = lax.axis_index("dp") * group
    meta = jnp.concatenate([root.reshape(1), doc_lengths]).astype(jnp.int32)
    dq, acc = attend("early", meta, mixed, heads=heads)
    dq, acc, rim_grad = attend("rim", meta, mixed, rim, dq, acc, heads=heads)
    back = from_behind(rim_grad, "dp", -1).astype(jnp.float32)
    dq, own = attend("late", meta, mixed, dq, acc, heads=heads)
    own = (own + back).astype(jnp.bfloat16)
    out_packed = jnp.concatenate([dq, own], axis=1).reshape(seq_count, rows, -1)
    returned = lax.all_to_all(out_packed, "seq", split_axis=0, concat_axis=0, tiled=True)
    qw = heads * HD
    grad_queries = returned[:, :, :qw].transpose(1, 0, 2).reshape(rows, seq_count * qw)

    def fold(part):
        part = part.astype(jnp.float32).reshape(KVH, repeat, rows, HD)
        return jnp.sum(part, axis=1).transpose(1, 0, 2).reshape(rows, KVH * HD).astype(jnp.bfloat16)

    grad_keys = fold(returned[:, :, qw : qw + HD])
    grad_values = fold(returned[:, :, qw + HD : qw + 2 * HD])
    return (grad_queries, grad_keys, grad_values)


def solution(mesh):
    return jax.shard_map(
        body,
        mesh=mesh,
        in_specs=(
            P(("dp", "seq"), None),
            P(("dp", "seq"), None),
            P(("dp", "seq"), None),
            P(("dp", "seq"), None),
            P(),
        ),
        out_specs=(P(("dp", "seq"), None), P(("dp", "seq"), None), P(("dp", "seq"), None)),
        check_vma=False,
    )
```
